128 devices in a mesh: group: 8 (over y_lo, x), head: 16 (over y_hi, z, core).
Axes of the slice: x: 4, y: 4 (y_hi: 2, y_lo: 2; y = y_hi * 2 + y_lo), z: 4, core: 2. Of those that a mesh axis runs over, the one named last changes fastest.
Arguments:
- symbol_lookup_table: bfloat16 [65536, 2048], P(None, 'head'), may hold values from -6 to 6
- joined_linear_maps: float32 [5, 2048, 2048], P(None, 'group', 'head'), may hold values from -0.125 to 0.125
- feedforward_lookup_map: float32 [2048, 7168], P('group', 'head'), may hold values from -0.125 to 0.125
- timeblend_result_map: float32 [2048, 2048], P('head', 'group'), may hold values from -0.125 to 0.125
- feedforward_content_map: float32 [7168, 2048], P('head', 'group'), may hold values from -0.0625 to 0.0625
- lag_blend_coefs: float32 [8, 2048], replicated, may hold values from 0 to 1
- blend_narrowing_map: bfloat16 [2048, 160], replicated, may hold values from -0.125 to 0.125
- blend_widening_maps: bfloat16 [5, 32, 2048], replicated, may hold values from -0.59765625 to 0.59765625
- fading_narrowing_map: bfloat16 [2048, 64], replicated, may hold values from -0.125 to 0.125
- fading_widening_map: bfloat16 [64, 2048], P(None, 'head'), as said below
- initial_fading_power: float32 [2048], P('head'), may hold values from -12 to -2.9
- present_symbol_extra: float32 [2048], P('head'), may hold values from -3 to 3
- attender_scaling_coefs: float32 [2048], P('head'), may hold values from 0.5 to 2
- active_cluster_sheets: int32 [8], replicated, may hold values from 2 to 4, as said below
- sheets_for_inquiry: int32 [7], replicated, may hold values from 2 to 7, as said below
- sheet_symbol_indices: int32 [24, 256], replicated, may hold values from 0 to 65535
Outputs:
- hidden_states: bfloat16 [8192, 2048], P('group', 'head')
- page_states: float32 [32, 32, 4096], P('group', 'head')
- shift_edges: float32 [32, 2, 2048], P('group', None, 'head')
The draws below stay inside these ranges and needn't reach their ends.
Inputs may be any that keep to these rules, and one draw needn't show every extreme that they name: `active_cluster_sheets`: they sum to 24; the two groups at one end of the axis, the first two or the last two, hold 4 pages each. `sheets_for_inquiry`: they sum to 24; the first page of every group but group 0 continues a request; the first or the last request holds 7 pages. `fading_widening_map`: each entry lies within 2.5 / sqrt(64) of zero.
All inputs are finite; a program needn't handle non-finite values.
Results may differ from the reference program's by a relative error of at most 0.017.
Values may be sent and summed in bfloat16 or wider, within the bound.
No kernel may reach another device: no remote copies, remote signals or barrier semaphores. Data moves between devices by JAX's collectives and lax.ppermute only.
A program may use at most 192 MiB of HBM per device.

```python
import math
import jax
import jax.numpy as jnp
import numpy as np
from jax import lax

FEATURE_SIZE = 2048
ATTENDER_TOTAL = 32
ATTENTION_DEPTH = 64
FF = 7168
VOCAB = 65536
MIXING_RANK = 32
DECAY_RANK = 64
PAGE = 256
SLOTS = 4
NPAGE = 24
N_GROUP = 8
N_HEAD = 16


def page_layout(key):
    base = jax.random.fold_in(key, 17)
    order_key, end_key, cut_key = jax.random.split(base, 3)
    group_number = jnp.arange(N_GROUP, dtype=jnp.int32)
    end_pick = jax.random.randint(end_key, (), 0, 2).astype(jnp.int32)
    raised = jnp.where(end_pick == 0, group_number < 2, group_number >= N_GROUP - 2)
    scores = jax.random.permutation(order_key, N_GROUP).astype(jnp.int32)
    scores = jnp.where(raised, N_GROUP + group_number, scores).astype(jnp.int32)
    ranking = jnp.argsort(jnp.argsort(scores, stable=True), stable=True).astype(jnp.int32)
    lowered = ranking < 2
    counts = (SLOTS - 1 + jnp.where(raised, 1, 0) - jnp.where(lowered, 1, 0)).astype(jnp.int32)
    offsets = jax.random.randint(cut_key, (N_GROUP,), 1, counts).astype(jnp.int32)
    offsets = jnp.where((end_pick == 0) & (group_number == 1), counts - 1, offsets)
    offsets = jnp.where((end_pick == 1) & (group_number == N_GROUP - 2), 1, offsets)
    offsets = jnp.where(group_number == 0, 0, jnp.where(group_number == N_GROUP - 1, counts, offsets)).astype(jnp.int32)
    requests = (counts[:-1] - offsets[:-1] + offsets[1:]).astype(jnp.int32)
    return (counts, requests)


def draw_active_cluster_sheets(key, part):
    counts, requests = page_layout(key)
    return counts


def draw_sheets_for_inquiry(key, part):
    counts, requests = page_layout(key)
    return requests


def draw_initial_fading_power(key, part):
    pick_key, fast_key, slow_key = jax.random.split(key, 3)
    fast_share = 0.5
    head_fast = jax.random.uniform(pick_key, (ATTENDER_TOTAL, 1)) < fast_share
    fast_rate = jax.random.uniform(fast_key, (ATTENDER_TOTAL, ATTENTION_DEPTH), minval=math.log(1.0 / 50.0), maxval=math.log(1.0 / 20.0))
    slow_rate = jax.random.uniform(slow_key, (ATTENDER_TOTAL, ATTENTION_DEPTH), minval=math.log(0.05), maxval=math.log(0.5)) - math.log(PAGE * (2 * SLOTS - 1))
    return jnp.where(head_fast, fast_rate, slow_rate).reshape(FEATURE_SIZE).astype(jnp.float32)


def draw_fading_widening_map(key, part):
    value_rows = jax.random.uniform(key, (DECAY_RANK, FEATURE_SIZE), minval=-1.0, maxval=1.0) * (2.5 / math.sqrt(DECAY_RANK))
    return value_rows.astype(jnp.float32).astype(jnp.bfloat16)


def with_ends(drawn, key, smallest, largest):
    longest = drawn.shape.index(max(drawn.shape))
    spots = []
    for shift in (0, 1):
        where = [jax.random.randint(jax.random.fold_in(key, axis), (), 0, length) for axis, length in enumerate(drawn.shape)]
        where[longest] = (where[longest] + shift) % drawn.shape[longest]
        spots.append(tuple(where))
    return drawn.at[spots[0]].set(smallest).at[spots[1]].set(largest)


def steps_of(stream_key, extent, pieces, least, high):
    def one(position, shards_of):
        steps = jax.random.uniform(jax.random.fold_in(jax.random.fold_in(stream_key, 6), position), (shards_of,), jnp.float32, least / len(pieces), high / len(pieces))
        return jnp.repeat(jnp.exp(steps), extent[position] // shards_of).reshape((-1,) + (1,) * (len(extent) - position - 1))

    loudness = one(*pieces[0])
    for cut in pieces[1:]:
        loudness = loudness * one(*cut)
    return loudness


def rank_bounds(number_of, skew):
    weights = [(1 << 20) // math.isqrt(standing ** skew) + 1 for standing in range(1, number_of + 1)]
    deviation = 1 + sum(weights) // (1 << 30)
    return np.cumsum(np.array([max(1, weight // deviation) for weight in weights]))


def skewed_ids(rng, dims, amount, skew):
    grid = rank_bounds(amount, skew)
    ticket = jax.random.randint(jax.random.fold_in(rng, 1), dims, 0, int(grid[amount - 1]))
    grade = jnp.searchsorted(jnp.asarray(grid, jnp.int32), ticket, side="right")
    return jax.random.permutation(jax.random.fold_in(rng, 2), amount)[grade].astype(jnp.int32)


def noise(stream_key, shape, deviation, reach, pieces=(), kind=jnp.bfloat16):
    factor_of = steps_of(stream_key, shape, pieces, -0.22, 0.18) if pieces else 1.0
    array = jax.random.normal(stream_key, shape, jnp.float32) * deviation * factor_of
    return jnp.minimum(jnp.maximum(array, -reach), reach).astype(kind)


def setup_inputs(seed: int = 0) -> dict:
    key_list = jax.random.split(jax.random.key(seed), 17)
    symbol_lookup_table = noise(key_list[0], (VOCAB, FEATURE_SIZE), 1.0, 6.0, ((1, 16),))
    joined_linear_maps = noise(key_list[1], (5, FEATURE_SIZE, FEATURE_SIZE), FEATURE_SIZE ** -0.5, 0.125, ((1, 8), (2, 16)), jnp.float32)
    feedforward_lookup_map = noise(key_list[2], (FEATURE_SIZE, FF), FEATURE_SIZE ** -0.5, 0.125, ((0, 8), (1, 16)), jnp.float32)
    timeblend_result_map = noise(key_list[3], (FEATURE_SIZE, FEATURE_SIZE), FEATURE_SIZE ** -0.5, 0.125, ((0, 16), (1, 8)), jnp.float32)
    feedforward_content_map = noise(key_list[4], (FF, FEATURE_SIZE), FF ** -0.5, 0.0625, ((0, 16), (1, 8)), jnp.float32)
    lag_blend_coefs = jnp.clip(jax.random.uniform(key_list[5], (8, FEATURE_SIZE), jnp.float32, 0.0, 1.0), 0.0, 1.0)
    blend_narrowing_map = noise(key_list[6], (FEATURE_SIZE, 5 * MIXING_RANK), FEATURE_SIZE ** -0.5, 0.125)
    blend_widening_maps = noise(key_list[7], (5, MIXING_RANK, FEATURE_SIZE), 0.1, 0.59765625)
    fading_narrowing_map = noise(key_list[8], (FEATURE_SIZE, DECAY_RANK), FEATURE_SIZE ** -0.5, 0.125)
    fading_widening_map = draw_fading_widening_map(jax.random.fold_in(key_list[16], 71), 0)
    initial_fading_power = draw_initial_fading_power(jax.random.fold_in(key_list[16], 71), 0)
    present_symbol_extra = noise(key_list[11], (FEATURE_SIZE,), 1.0, 3.0, ((0, 16),), jnp.float32)
    attender_scaling_coefs = jnp.clip(jnp.exp(math.log(2.0) - 1.3862944 * jax.random.uniform(key_list[12], (FEATURE_SIZE,), jnp.float32) ** steps_of(key_list[12], (FEATURE_SIZE,), ((0, 16),), -0.2, 0.2)), 0.5, 2.0)
    active_cluster_sheets = draw_active_cluster_sheets(jax.random.fold_in(key_list[16], 71), 0)
    sheets_for_inquiry = draw_sheets_for_inquiry(jax.random.fold_in(key_list[16], 71), 0)
    sheet_symbol_indices = with_ends(skewed_ids(key_list[15], (NPAGE, PAGE), VOCAB, 2), jax.random.fold_in(key_list[15], 3), 0, VOCAB - 1).astype(jnp.int32)
    return dict(symbol_lookup_table=symbol_lookup_table, joined_linear_maps=joined_linear_maps, feedforward_lookup_map=feedforward_lookup_map, timeblend_result_map=timeblend_result_map, feedforward_content_map=feedforward_content_map, lag_blend_coefs=lag_blend_coefs, blend_narrowing_map=blend_narrowing_map, blend_widening_maps=blend_widening_maps, fading_narrowing_map=fading_narrowing_map, fading_widening_map=fading_widening_map, initial_fading_power=initial_fading_power, present_symbol_extra=present_symbol_extra, attender_scaling_coefs=attender_scaling_coefs, active_cluster_sheets=active_cluster_sheets, sheets_for_inquiry=sheets_for_inquiry, sheet_symbol_indices=sheet_symbol_indices)


EXACT_ARITHMETIC = lax.Precision.HIGHEST
LAYER_EPS = 1e-05
GROUP_EPS = 0.00064

def layer_norm(value_rows):
    value_rows = value_rows.astype(jnp.float32)
    centered = value_rows - lax.optimization_barrier(jnp.mean(value_rows, axis=-1, keepdims=True))
    return centered * lax.rsqrt(lax.optimization_barrier(jnp.mean(centered * centered, axis=-1, keepdims=True)) + LAYER_EPS)

def mixed_inputs(current, previous, lag_blend_coefs, blend_narrowing_map, blend_widening_maps):
    delta_rows = previous - current
    seeded = (current + delta_rows * lag_blend_coefs[0]).astype(jnp.bfloat16)
    low_rank = jnp.tanh(jnp.dot(seeded, blend_narrowing_map, preferred_element_type=jnp.float32)).astype(jnp.bfloat16)
    rank_width = blend_widening_maps.shape[1]
    result_lines = []
    for number in range(5):
        column_part = low_rank[:, number * rank_width:(number + 1) * rank_width]
        offset = jnp.dot(column_part, blend_widening_maps[number], preferred_element_type=jnp.float32)
        result_lines.append((current + delta_rows * (lag_blend_coefs[number + 1] + offset)).astype(jnp.bfloat16))
    return result_lines

def log_decay(mixed_decay, fading_narrowing_map, fading_widening_map, initial_fading_power):
    hidden_low = jnp.tanh(jnp.dot(mixed_decay, fading_narrowing_map, preferred_element_type=jnp.float32)).astype(jnp.bfloat16)
    return -jnp.exp(initial_fading_power + jnp.dot(hidden_low, fading_widening_map, preferred_element_type=jnp.float32))

def group_norm(value_rows):
    shaped = value_rows.reshape(value_rows.shape[0], -1, ATTENTION_DEPTH)
    centered = shaped - lax.optimization_barrier(jnp.mean(shaped, axis=-1, keepdims=True))
    normed = centered * lax.rsqrt(lax.optimization_barrier(jnp.mean(centered * centered, axis=-1, keepdims=True)) + GROUP_EPS)
    return normed.reshape(value_rows.shape)

def blocked_sum(left_side, right_side, block_count):
    inner_width = left_side.shape[1] // block_count
    left_blocks = left_side.reshape(left_side.shape[0], block_count, inner_width).astype(jnp.float32)
    right_blocks = right_side.reshape(block_count, inner_width, right_side.shape[1]).astype(jnp.float32)
    partials = jnp.einsum('pqc,qcd->pqd', left_blocks, right_blocks, precision=EXACT_ARITHMETIC)
    partials = lax.optimization_barrier(partials.astype(jnp.bfloat16))
    return lax.optimization_barrier(jnp.sum(partials.astype(jnp.float32), axis=1))

def memory_evolution(acceptance_lines, present_lookups, present_contents, fading_multipliers, attender_extra, sequential_sweep):

    def advance(retained_memory, inputs):
        present_asker, key_now, value_now, decay_now = inputs
        lookup_content_product = key_now[:, :, None] * value_now[:, None, :]
        sublevel_result = jnp.einsum('ws,wsm->wm', present_asker, retained_memory + attender_extra[:, :, None] * lookup_content_product, precision=EXACT_ARITHMETIC)
        retained_memory = jnp.exp(decay_now)[:, :, None] * retained_memory + lookup_content_product
        return (retained_memory, sublevel_result)
    return lax.scan(advance, sequential_sweep, (acceptance_lines, present_lookups, present_contents, fading_multipliers))

def reference(symbol_lookup_table, joined_linear_maps, feedforward_lookup_map, timeblend_result_map, feedforward_content_map, lag_blend_coefs, blend_narrowing_map, blend_widening_maps, fading_narrowing_map, fading_widening_map, initial_fading_power, present_symbol_extra, attender_scaling_coefs, active_cluster_sheets, sheets_for_inquiry, sheet_symbol_indices):
    projections = joined_linear_maps.astype(jnp.bfloat16)
    key_weight = feedforward_lookup_map.astype(jnp.bfloat16)
    output_weight = timeblend_result_map.astype(jnp.bfloat16)
    value_weight = feedforward_content_map.astype(jnp.bfloat16)
    request_first = (jnp.cumsum(sheets_for_inquiry) - sheets_for_inquiry).astype(jnp.int32)
    page_number = jnp.arange(NPAGE, dtype=jnp.int32)
    begins = jnp.any(page_number[:, None] == request_first[None, :], axis=1)
    carry_on = jnp.where(begins, 0.0, 1.0).astype(jnp.float32)
    before_token = jnp.concatenate([sheet_symbol_indices[:1, 0], sheet_symbol_indices[:-1, -1]])
    attender_extra = present_symbol_extra.reshape(ATTENDER_TOTAL, ATTENTION_DEPTH)

    def attender_split_layout(value_rows):
        return value_rows.reshape(PAGE, ATTENDER_TOTAL, ATTENTION_DEPTH)

    def page_step(retained_memory, inputs):
        sequential_sweep, last_row = retained_memory
        tokens_here, token_before, keep_going = inputs
        sequential_sweep = sequential_sweep * keep_going
        last_row = last_row * keep_going
        embedded = jnp.take(symbol_lookup_table, tokens_here, axis=0)
        current = layer_norm(embedded)
        edge_first = layer_norm(jnp.take(symbol_lookup_table, token_before[None], axis=0)) * keep_going
        previous = jnp.concatenate([edge_first, current[:-1]], axis=0)
        mixed_decay, mixed_key, mixed_value, mixed_query, mixed_gate = mixed_inputs(current, previous, lag_blend_coefs, blend_narrowing_map, blend_widening_maps)
        fading_multipliers = log_decay(mixed_decay, fading_narrowing_map, fading_widening_map, initial_fading_power)
        acceptance_lines = jnp.dot(mixed_query, projections[0], preferred_element_type=jnp.float32)
        present_lookups = jnp.dot(mixed_key, projections[1], preferred_element_type=jnp.float32)
        present_contents = jnp.dot(mixed_value, projections[2], preferred_element_type=jnp.float32)
        gating = jax.nn.silu(jnp.dot(mixed_gate, projections[3], preferred_element_type=jnp.float32))
        sequential_sweep, result_lines = memory_evolution(attender_split_layout(acceptance_lines), attender_split_layout(present_lookups), attender_split_layout(present_contents), attender_split_layout(fading_multipliers), attender_extra, sequential_sweep)
        attended = result_lines.reshape(PAGE, FEATURE_SIZE)
        normed = (group_norm(attended) * attender_scaling_coefs * gating).astype(jnp.bfloat16)
        mixer_total = blocked_sum(normed, output_weight, N_HEAD)
        residual = (embedded.astype(jnp.float32) + mixer_total).astype(jnp.bfloat16)
        channel_in = layer_norm(residual)
        channel_prev = jnp.concatenate([last_row[None, :], channel_in[:-1]], axis=0)
        channel_delta = channel_prev - channel_in
        key_input = (channel_in + channel_delta * lag_blend_coefs[6]).astype(jnp.bfloat16)
        gate_input = (channel_in + channel_delta * lag_blend_coefs[7]).astype(jnp.bfloat16)
        squared = jnp.square(jax.nn.relu(jnp.dot(key_input, key_weight, preferred_element_type=jnp.float32))).astype(jnp.bfloat16)
        channel = blocked_sum(squared, value_weight, N_HEAD)
        gate_two = jax.nn.sigmoid(jnp.dot(gate_input, projections[4], preferred_element_type=jnp.float32))
        hidden = (residual.astype(jnp.float32) + gate_two * channel).astype(jnp.bfloat16)
        edge_pair = jnp.stack([current[-1], channel_in[-1]])
        return ((sequential_sweep, channel_in[-1]), (hidden, sequential_sweep.reshape(ATTENDER_TOTAL, ATTENTION_DEPTH * ATTENTION_DEPTH), edge_pair))
    start_carry = (jnp.zeros((ATTENDER_TOTAL, ATTENTION_DEPTH, ATTENTION_DEPTH), jnp.float32), jnp.zeros((FEATURE_SIZE,), jnp.float32))
    final_carry, (hidden_pages, state_pages, edge_pages) = lax.scan(page_step, start_carry, (sheet_symbol_indices, before_token, carry_on))
    group_first = (jnp.cumsum(active_cluster_sheets) - active_cluster_sheets).astype(jnp.int32)
    slot_group = jnp.arange(N_GROUP * SLOTS, dtype=jnp.int32) // SLOTS
    slot_place = jnp.arange(N_GROUP * SLOTS, dtype=jnp.int32) % SLOTS
    slot_live = slot_place < jnp.take(active_cluster_sheets, slot_group)
    slot_page = jnp.where(slot_live, jnp.take(group_first, slot_group) + slot_place, 0).astype(jnp.int32)
    hidden_slots = jnp.take(hidden_pages, slot_page, axis=0)
    hidden_states = jnp.where(slot_live[:, None, None], hidden_slots, jnp.zeros_like(hidden_slots)).reshape(N_GROUP * SLOTS * PAGE, FEATURE_SIZE)
    state_slots = jnp.take(state_pages, slot_page, axis=0)
    page_states = jnp.where(slot_live[:, None, None], state_slots, jnp.zeros_like(state_slots))
    edge_slots = jnp.take(edge_pages, slot_page, axis=0)
    shift_edges = jnp.where(slot_live[:, None, None], edge_slots, jnp.zeros_like(edge_slots))
    return (hidden_states, page_states, shift_edges)
```

```python
import jax
import jax.numpy as jnp
from jax import lax
from jax.sharding import PartitionSpec as P

ATTENTION_DEPTH = 64
PAGE = 256
SLOTS = 4
BLOCK = 128


EXACT_ARITHMETIC = lax.Precision.HIGHEST
LAYER_EPS = 1e-05
GROUP_EPS = 0.00064


def passed_along(value, axis, steps):
    count = lax.axis_size(axis)
    initial, last = (max(0, -steps), min(count, count - steps))
    return lax.ppermute(value, axis, [(source, source + steps) for source in range(initial, last)])


def layer_norm(value_rows):
    value_rows = value_rows.astype(jnp.float32)
    centered = value_rows - jnp.mean(value_rows, axis=-1, keepdims=True)
    return centered * lax.rsqrt(jnp.mean(centered * centered, axis=-1, keepdims=True) + LAYER_EPS)


def mixed_inputs(current, previous, lag_blend_coefs, blend_narrowing_map, blend_widening_maps):
    delta_rows = previous - current
    seeded = (current + delta_rows * lag_blend_coefs[0]).astype(jnp.bfloat16)
    low_rank = jnp.tanh(
        jnp.dot(seeded, blend_narrowing_map, preferred_element_type=jnp.float32)
    ).astype(jnp.bfloat16)
    rank_width = blend_widening_maps.shape[1]
    result_lines = []
    for number in range(5):
        column_part = low_rank[:, number * rank_width : (number + 1) * rank_width]
        offset = jnp.dot(
            column_part, blend_widening_maps[number], preferred_element_type=jnp.float32
        )
        result_lines.append(
            (current + delta_rows * (lag_blend_coefs[number + 1] + offset)).astype(jnp.bfloat16)
        )
    return result_lines


def log_decay(mixed_decay, fading_narrowing_map, fading_widening_map, initial_fading_power):
    hidden_low = jnp.tanh(
        jnp.dot(mixed_decay, fading_narrowing_map, preferred_element_type=jnp.float32)
    ).astype(jnp.bfloat16)
    return -jnp.exp(
        initial_fading_power
        + jnp.dot(hidden_low, fading_widening_map, preferred_element_type=jnp.float32)
    )


def group_norm(value_rows):
    shaped = value_rows.reshape(value_rows.shape[0], -1, ATTENTION_DEPTH)
    centered = shaped - jnp.mean(shaped, axis=-1, keepdims=True)
    normed = centered * lax.rsqrt(jnp.mean(centered * centered, axis=-1, keepdims=True) + GROUP_EPS)
    return normed.reshape(value_rows.shape)


def per_device(
    symbol_lookup_table,
    joined_linear_maps,
    feedforward_lookup_map,
    timeblend_result_map,
    feedforward_content_map,
    lag_blend_coefs,
    blend_narrowing_map,
    blend_widening_maps,
    fading_narrowing_map,
    fading_widening_map,
    initial_fading_power,
    present_symbol_extra,
    attender_scaling_coefs,
    active_cluster_sheets,
    sheets_for_inquiry,
    sheet_symbol_indices,
):
    group_count = lax.axis_size("group")
    group_here = lax.axis_index("group")
    head_here = lax.axis_index("head")
    features_on_shard = present_symbol_extra.shape[0]
    attenders_on_shard = features_on_shard // ATTENTION_DEPTH
    slot_rows = SLOTS * PAGE
    full_width = lag_blend_coefs.shape[1]
    group_number = jnp.arange(group_count, dtype=jnp.int32)
    pick_group = group_number == group_here
    live_count = jnp.sum(jnp.where(pick_group, active_cluster_sheets, 0))
    group_first = jnp.cumsum(active_cluster_sheets) - active_cluster_sheets
    first_page = jnp.sum(jnp.where(pick_group, group_first, 0))
    slot_number = jnp.arange(SLOTS, dtype=jnp.int32)
    slot_live = slot_number < live_count
    request_first = jnp.cumsum(sheets_for_inquiry) - sheets_for_inquiry
    page_here = first_page + slot_number
    begins = jnp.any(page_here[:, None] == request_first[None, :], axis=1)
    continues = jnp.where(slot_live & jnp.logical_not(begins), 1.0, 0.0).astype(jnp.float32)
    safe_page = jnp.where(slot_live, page_here, 0)
    tokens_here = jnp.take(sheet_symbol_indices, safe_page, axis=0)
    before_token = jnp.take(sheet_symbol_indices[:, -1], jnp.maximum(safe_page - 1, 0))
    edge_pad = jnp.concatenate([before_token, jnp.zeros((8 - SLOTS,), before_token.dtype)])
    all_tokens = jnp.concatenate([tokens_here.reshape(-1), edge_pad])
    own_rows = jnp.take(symbol_lookup_table, all_tokens, axis=0)
    gathered_rows = lax.all_gather(own_rows, "head", axis=1, tiled=True)
    embedded = gathered_rows[:slot_rows]
    edge_rows = gathered_rows[slot_rows : slot_rows + SLOTS]
    map_count = joined_linear_maps.shape[0]
    first_pack = jnp.concatenate(
        [joined_linear_maps, timeblend_result_map.T[None]], axis=0
    ).astype(jnp.bfloat16)
    second_pack = jnp.stack(
        [feedforward_lookup_map, feedforward_content_map.T], axis=0
    ).astype(jnp.bfloat16)
    first_full = lax.all_gather(first_pack, "group", axis=1, tiled=True)
    second_full = lax.all_gather(second_pack, "group", axis=1, tiled=True)
    projections = first_full[:map_count]
    output_weight_t = first_full[map_count]
    key_weight = second_full[0]
    value_weight_t = second_full[1]
    current = layer_norm(embedded)
    edge_first = layer_norm(edge_rows) * continues[:, None]
    current_pages = current.reshape(SLOTS, PAGE, full_width)
    previous = jnp.concatenate([edge_first[:, None, :], current_pages[:, :-1, :]], axis=1).reshape(
        slot_rows, full_width
    )
    mixed_decay, mixed_key, mixed_value, mixed_query, mixed_gate = mixed_inputs(
        current, previous, lag_blend_coefs, blend_narrowing_map, blend_widening_maps
    )
    fading_multipliers = log_decay(
        mixed_decay, fading_narrowing_map, fading_widening_map, initial_fading_power
    )
    acceptance_lines = jnp.dot(mixed_query, projections[0], preferred_element_type=jnp.float32)
    present_lookups = jnp.dot(mixed_key, projections[1], preferred_element_type=jnp.float32)
    present_contents = jnp.dot(mixed_value, projections[2], preferred_element_type=jnp.float32)
    gate_raw = jnp.dot(mixed_gate, projections[3], preferred_element_type=jnp.float32)
    gating = jax.nn.silu(gate_raw)
    blocks = slot_rows // BLOCK
    per_page = PAGE // BLOCK

    def to_blocks(value_rows):
        return value_rows.reshape(blocks, BLOCK, attenders_on_shard, ATTENTION_DEPTH).transpose(
            0, 2, 1, 3
        )

    block_index = jnp.arange(blocks, dtype=jnp.int32)
    block_start = block_index % per_page == 0
    block_slot = block_index // per_page
    slot_keep = continues * (slot_number > 0)
    keep_state = jnp.where(block_start, jnp.take(slot_keep, block_slot), 1.0)
    keep_factor = jnp.where(block_start, jnp.take(continues, block_slot), 1.0)
    attender_extra = present_symbol_extra.reshape(attenders_on_shard, ATTENTION_DEPTH)
    strictly_lower = jnp.arange(BLOCK)[:, None] > jnp.arange(BLOCK)[None, :]

    askers_b = to_blocks(acceptance_lines)
    lookups_b = to_blocks(present_lookups)
    values_b = to_blocks(present_contents)
    decay_b = to_blocks(fading_multipliers)
    inclusive = jnp.cumsum(decay_b, axis=2)
    exclusive = inclusive - decay_b
    query_scaled = askers_b * jnp.exp(exclusive)
    key_scaled = lookups_b * jnp.exp(-inclusive)
    scores = jnp.einsum("bhts,bhus->bhtu", query_scaled, key_scaled, precision=EXACT_ARITHMETIC)
    scores = jnp.where(strictly_lower, scores, 0.0)
    selfpair_contribution = jnp.sum(askers_b * attender_extra[None, :, None, :] * lookups_b, axis=3)
    intra = (
        jnp.einsum("bhtu,bhuj->bhtj", scores, values_b, precision=EXACT_ARITHMETIC)
        + selfpair_contribution[..., None] * values_b
    )
    block_total = inclusive[:, :, -1, :]
    block_decay = jnp.exp(block_total)
    key_end = lookups_b * jnp.exp(block_total[:, :, None, :] - inclusive)
    block_kv = jnp.einsum("bhts,bhtj->bhsj", key_end, values_b, precision=EXACT_ARITHMETIC)
    sweep = jnp.zeros((attenders_on_shard, ATTENTION_DEPTH, ATTENTION_DEPTH), jnp.float32)
    factor = jnp.ones((attenders_on_shard, ATTENTION_DEPTH), jnp.float32)
    starts, factors_before, ends, factors_after = [], [], [], []
    for number in range(blocks):
        sweep = sweep * keep_state[number]
        factor = factor * keep_factor[number]
        starts.append(sweep)
        factors_before.append(factor)
        sweep = block_decay[number][:, :, None] * sweep + block_kv[number]
        factor = factor * block_decay[number]
        ends.append(sweep)
        factors_after.append(factor)
    block_out = intra + jnp.einsum(
        "bhts,bhsj->bhtj", query_scaled, jnp.stack(starts), precision=EXACT_ARITHMETIC
    )
    carry_rows = query_scaled * jnp.stack(factors_before)[:, :, None, :]
    block_states = jnp.stack(ends)
    block_factors = jnp.stack(factors_after)
    page_end = block_states[per_page - 1 :: per_page]
    page_factor = block_factors[per_page - 1 :: per_page]
    last_pick = (slot_number == live_count - 1).astype(jnp.float32)
    leaving_state = jnp.einsum("s,shij->hij", last_pick, page_end, precision=EXACT_ARITHMETIC)
    leaving_factor = jnp.einsum("s,shi->hi", last_pick, page_factor, precision=EXACT_ARITHMETIC)

    leaving_pack = jnp.concatenate([leaving_state, leaving_factor[:, None, :]], axis=1)
    every_pack = lax.all_gather(leaving_pack, "group", axis=0, tiled=False)
    incoming = jnp.zeros_like(leaving_state)
    for number in range(group_count - 1):
        composed = every_pack[number, :, ATTENTION_DEPTH, :][:, :, None] * incoming + every_pack[
            number, :, :ATTENTION_DEPTH, :
        ]
        incoming = jnp.where(number < group_here, composed, incoming)
    block_out = block_out + jnp.einsum(
        "bhts,hsj->bhtj", carry_rows, incoming, precision=EXACT_ARITHMETIC
    )
    page_end = page_end + page_factor[:, :, :, None] * incoming[None]
    attended = block_out.transpose(0, 2, 1, 3).reshape(slot_rows, features_on_shard)
    normed = (group_norm(attended) * attender_scaling_coefs * gating).astype(jnp.bfloat16)
    mixer_total = lax.psum(
        lax.dot_general(
            normed, output_weight_t, (((1,), (1,)), ((), ())), preferred_element_type=jnp.float32
        ).astype(jnp.bfloat16),
        "head",
    ).astype(jnp.float32)
    residual = (embedded.astype(jnp.float32) + mixer_total).astype(jnp.bfloat16)
    last_residual = lax.dynamic_slice_in_dim(residual, live_count * PAGE - 1, 1, 0)
    arriving = passed_along(last_residual, "group", 1)
    channel_in = layer_norm(residual)
    channel_pages = channel_in.reshape(SLOTS, PAGE, full_width)
    edge_two = (
        jnp.concatenate([layer_norm(arriving), channel_pages[:-1, -1, :]], axis=0)
        * continues[:, None]
    )
    channel_prev = jnp.concatenate(
        [edge_two[:, None, :], channel_pages[:, :-1, :]], axis=1
    ).reshape(slot_rows, full_width)
    channel_delta = channel_prev - channel_in
    key_input = (channel_in + channel_delta * lag_blend_coefs[6]).astype(jnp.bfloat16)
    gate_input = (channel_in + channel_delta * lag_blend_coefs[7]).astype(jnp.bfloat16)
    gate_raw_two = jnp.dot(gate_input, projections[4], preferred_element_type=jnp.float32)
    key_raw = jnp.dot(key_input, key_weight, preferred_element_type=jnp.float32)
    squared = jnp.square(jax.nn.relu(key_raw)).astype(jnp.bfloat16)
    channel = lax.psum_scatter(
        lax.dot_general(
            squared, value_weight_t, (((1,), (1,)), ((), ())), preferred_element_type=jnp.float32
        ).astype(jnp.bfloat16),
        "head",
        scatter_dimension=1,
        tiled=True,
    ).astype(jnp.float32)
    gate_two = jax.nn.sigmoid(gate_raw_two)
    residual_local = lax.dynamic_slice_in_dim(
        residual, head_here * features_on_shard, features_on_shard, 1
    )
    hidden = (residual_local.astype(jnp.float32) + gate_two * channel).astype(jnp.bfloat16)
    row_live = jnp.repeat(slot_live, PAGE)
    hidden_out = jnp.where(row_live[:, None], hidden, jnp.zeros_like(hidden))
    state_out = page_end.reshape(SLOTS, attenders_on_shard, ATTENTION_DEPTH * ATTENTION_DEPTH)
    state_out = jnp.where(slot_live[:, None, None], state_out, jnp.zeros_like(state_out))
    first_edge = lax.dynamic_slice_in_dim(
        current_pages[:, -1, :], head_here * features_on_shard, features_on_shard, 1
    )
    second_edge = lax.dynamic_slice_in_dim(
        channel_pages[:, -1, :], head_here * features_on_shard, features_on_shard, 1
    )
    edge_out = jnp.stack([first_edge, second_edge], axis=1)
    edge_out = jnp.where(slot_live[:, None, None], edge_out, jnp.zeros_like(edge_out))
    return (hidden_out, state_out, edge_out)


def solution(mesh):
    in_specs = (
        P(None, "head"),
        P(None, "group", "head"),
        P("group", "head"),
        P("head", "group"),
        P("head", "group"),
        P(),
        P(),
        P(),
        P(),
        P(None, "head"),
        P("head"),
        P("head"),
        P("head"),
        P(),
        P(),
        P(),
    )
    out_specs = (P("group", "head"), P("group", "head", None), P("group", None, "head"))
    return jax.shard_map(
        per_device, mesh=mesh, in_specs=in_specs, out_specs=out_specs, check_vma=False
    )
```

```python
import jax
import jax.numpy as jnp
from jax import lax
from jax.sharding import PartitionSpec as P

ATTENTION_DEPTH = 64
PAGE = 256
SLOTS = 4
BLOCK = 128


EXACT_ARITHMETIC = lax.Precision.HIGHEST
LAYER_EPS = 1e-05
GROUP_EPS = 0.00064


def passed_along(value, axis, steps):
    count = lax.axis_size(axis)
    initial, last = (max(0, -steps), min(count, count - steps))
    return lax.ppermute(value, axis, [(source, source + steps) for source in range(initial, last)])


def layer_norm(value_rows):
    value_rows = value_rows.astype(jnp.float32)
    centered = value_rows - jnp.mean(value_rows, axis=-1, keepdims=True)
    return centered * lax.rsqrt(jnp.mean(centered * centered, axis=-1, keepdims=True) + LAYER_EPS)


def mixed_inputs(current, previous, lag_blend_coefs, blend_narrowing_map, blend_widening_maps):
    delta_rows = previous - current
    seeded = (current + delta_rows * lag_blend_coefs[0]).astype(jnp.bfloat16)
    low_rank = jnp.tanh(
        jnp.dot(seeded, blend_narrowing_map, preferred_element_type=jnp.float32)
    ).astype(jnp.bfloat16)
    rank_width = blend_widening_maps.shape[1]
    result_lines = []
    for number in range(5):
        column_part = low_rank[:, number * rank_width : (number + 1) * rank_width]
        offset = jnp.dot(
            column_part, blend_widening_maps[number], preferred_element_type=jnp.float32
        )
        result_lines.append(
            (current + delta_rows * (lag_blend_coefs[number + 1] + offset)).astype(jnp.bfloat16)
        )
    return result_lines


def log_decay(mixed_decay, fading_narrowing_map, fading_widening_map, initial_fading_power):
    hidden_low = jnp.tanh(
        jnp.dot(mixed_decay, fading_narrowing_map, preferred_element_type=jnp.float32)
    ).astype(jnp.bfloat16)
    return -jnp.exp(
        initial_fading_power
        + jnp.dot(hidden_low, fading_widening_map, preferred_element_type=jnp.float32)
    )


def group_norm(value_rows):
    shaped = value_rows.reshape(value_rows.shape[0], -1, ATTENTION_DEPTH)
    centered = shaped - jnp.mean(shaped, axis=-1, keepdims=True)
    normed = centered * lax.rsqrt(jnp.mean(centered * centered, axis=-1, keepdims=True) + GROUP_EPS)
    return normed.reshape(value_rows.shape)


def per_device(
    symbol_lookup_table,
    joined_linear_maps,
    feedforward_lookup_map,
    timeblend_result_map,
    feedforward_content_map,
    lag_blend_coefs,
    blend_narrowing_map,
    blend_widening_maps,
    fading_narrowing_map,
    fading_widening_map,
    initial_fading_power,
    present_symbol_extra,
    attender_scaling_coefs,
    active_cluster_sheets,
    sheets_for_inquiry,
    sheet_symbol_indices,
):
    group_count = lax.axis_size("group")
    group_here = lax.axis_index("group")
    head_here = lax.axis_index("head")
    features_on_shard = present_symbol_extra.shape[0]
    attenders_on_shard = features_on_shard // ATTENTION_DEPTH
    slot_rows = SLOTS * PAGE
    full_width = lag_blend_coefs.shape[1]
    group_number = jnp.arange(group_count, dtype=jnp.int32)
    pick_group = group_number == group_here
    live_count = jnp.sum(jnp.where(pick_group, active_cluster_sheets, 0))
    group_first = jnp.cumsum(active_cluster_sheets) - active_cluster_sheets
    first_page = jnp.sum(jnp.where(pick_group, group_first, 0))
    slot_number = jnp.arange(SLOTS, dtype=jnp.int32)
    slot_live = slot_number < live_count
    request_first = jnp.cumsum(sheets_for_inquiry) - sheets_for_inquiry
    page_here = first_page + slot_number
    begins = jnp.any(page_here[:, None] == request_first[None, :], axis=1)
    continues = jnp.where(slot_live & jnp.logical_not(begins), 1.0, 0.0).astype(jnp.float32)
    safe_page = jnp.where(slot_live, page_here, 0)
    tokens_here = jnp.take(sheet_symbol_indices, safe_page, axis=0)
    before_token = jnp.take(sheet_symbol_indices[:, -1], jnp.maximum(safe_page - 1, 0))
    edge_pad = jnp.concatenate([before_token, jnp.zeros((8 - SLOTS,), before_token.dtype)])
    all_tokens = jnp.concatenate([tokens_here.reshape(-1), edge_pad])
    own_rows = jnp.take(symbol_lookup_table, all_tokens, axis=0)
    gathered_rows = lax.all_gather(own_rows, "head", axis=1, tiled=True)
    embedded = gathered_rows[:slot_rows]
    edge_rows = gathered_rows[slot_rows : slot_rows + SLOTS]
    map_count = joined_linear_maps.shape[0]
    first_pack = jnp.concatenate(
        [joined_linear_maps, timeblend_result_map.T[None]], axis=0
    ).astype(jnp.bfloat16)
    second_pack = jnp.stack(
        [feedforward_lookup_map, feedforward_content_map.T], axis=0
    ).astype(jnp.bfloat16)
    first_pack, _ = lax.optimization_barrier((first_pack, gathered_rows))
    first_full = lax.all_gather(first_pack, "group", axis=1, tiled=True)
    second_pack, _ = lax.optimization_barrier((second_pack, first_full))
    second_full = lax.all_gather(second_pack, "group", axis=1, tiled=True)
    projections = first_full[:map_count]
    output_weight_t = first_full[map_count]
    key_weight = second_full[0]
    value_weight_t = second_full[1]
    current = layer_norm(embedded)
    edge_first = layer_norm(edge_rows) * continues[:, None]
    current_pages = current.reshape(SLOTS, PAGE, full_width)
    previous = jnp.concatenate([edge_first[:, None, :], current_pages[:, :-1, :]], axis=1).reshape(
        slot_rows, full_width
    )
    mixed_decay, mixed_key, mixed_value, mixed_query, mixed_gate = mixed_inputs(
        current, previous, lag_blend_coefs, blend_narrowing_map, blend_widening_maps
    )
    fading_multipliers = log_decay(
        mixed_decay, fading_narrowing_map, fading_widening_map, initial_fading_power
    )
    acceptance_lines = jnp.dot(mixed_query, projections[0], preferred_element_type=jnp.float32)
    present_lookups = jnp.dot(mixed_key, projections[1], preferred_element_type=jnp.float32)
    present_contents = jnp.dot(mixed_value, projections[2], preferred_element_type=jnp.float32)
    gate_raw = jnp.dot(mixed_gate, projections[3], preferred_element_type=jnp.float32)
    gating = jax.nn.silu(gate_raw)
    blocks = slot_rows // BLOCK
    per_page = PAGE // BLOCK

    def to_blocks(value_rows):
        return value_rows.reshape(blocks, BLOCK, attenders_on_shard, ATTENTION_DEPTH).transpose(
            0, 2, 1, 3
        )

    block_index = jnp.arange(blocks, dtype=jnp.int32)
    block_start = block_index % per_page == 0
    block_slot = block_index // per_page
    slot_keep = continues * (slot_number > 0)
    keep_state = jnp.where(block_start, jnp.take(slot_keep, block_slot), 1.0)
    keep_factor = jnp.where(block_start, jnp.take(continues, block_slot), 1.0)
    attender_extra = present_symbol_extra.reshape(attenders_on_shard, ATTENTION_DEPTH)
    strictly_lower = jnp.arange(BLOCK)[:, None] > jnp.arange(BLOCK)[None, :]

    askers_b = to_blocks(acceptance_lines)
    lookups_b = to_blocks(present_lookups)
    values_b = to_blocks(present_contents)
    decay_b = to_blocks(fading_multipliers)
    inclusive = jnp.cumsum(decay_b, axis=2)
    exclusive = inclusive - decay_b
    query_scaled = askers_b * jnp.exp(exclusive)
    key_scaled = lookups_b * jnp.exp(-inclusive)
    scores = jnp.einsum("bhts,bhus->bhtu", query_scaled, key_scaled, precision=EXACT_ARITHMETIC)
    scores = jnp.where(strictly_lower, scores, 0.0)
    selfpair_contribution = jnp.sum(askers_b * attender_extra[None, :, None, :] * lookups_b, axis=3)
    intra = (
        jnp.einsum("bhtu,bhuj->bhtj", scores, values_b, precision=EXACT_ARITHMETIC)
        + selfpair_contribution[..., None] * values_b
    )
    block_total = inclusive[:, :, -1, :]
    block_decay = jnp.exp(block_total)
    key_end = lookups_b * jnp.exp(block_total[:, :, None, :] - inclusive)
    block_kv = jnp.einsum("bhts,bhtj->bhsj", key_end, values_b, precision=EXACT_ARITHMETIC)
    sweep = jnp.zeros((attenders_on_shard, ATTENTION_DEPTH, ATTENTION_DEPTH), jnp.float32)
    factor = jnp.ones((attenders_on_shard, ATTENTION_DEPTH), jnp.float32)
    starts, factors_before, ends, factors_after = [], [], [], []
    for number in range(blocks):
        sweep = sweep * keep_state[number]
        factor = factor * keep_factor[number]
        starts.append(sweep)
        factors_before.append(factor)
        sweep = block_decay[number][:, :, None] * sweep + block_kv[number]
        factor = factor * block_decay[number]
        ends.append(sweep)
        factors_after.append(factor)
    block_out = intra + jnp.einsum(
        "bhts,bhsj->bhtj", query_scaled, jnp.stack(starts), precision=EXACT_ARITHMETIC
    )
    carry_rows = query_scaled * jnp.stack(factors_before)[:, :, None, :]
    block_states = jnp.stack(ends)
    block_factors = jnp.stack(factors_after)
    page_end = block_states[per_page - 1 :: per_page]
    page_factor = block_factors[per_page - 1 :: per_page]
    last_pick = (slot_number == live_count - 1).astype(jnp.float32)
    leaving_state = jnp.einsum("s,shij->hij", last_pick, page_end, precision=EXACT_ARITHMETIC)
    leaving_factor = jnp.einsum("s,shi->hi", last_pick, page_factor, precision=EXACT_ARITHMETIC)

    leaving_pack = jnp.concatenate([leaving_state, leaving_factor[:, None, :]], axis=1)
    arrivals = [passed_along(leaving_pack, "group", distance) for distance in range(1, group_count)]
    incoming = jnp.zeros_like(leaving_state)
    for arrival in reversed(arrivals):
        incoming = arrival[:, ATTENTION_DEPTH, :][:, :, None] * incoming + arrival[:, :ATTENTION_DEPTH, :]
    block_out = block_out + jnp.einsum(
        "bhts,hsj->bhtj", carry_rows, incoming, precision=EXACT_ARITHMETIC
    )
    page_end = page_end + page_factor[:, :, :, None] * incoming[None]
    attended = block_out.transpose(0, 2, 1, 3).reshape(slot_rows, features_on_shard)
    normed = (group_norm(attended) * attender_scaling_coefs * gating).astype(jnp.bfloat16)
    mixer_partial = lax.dot_general(
        normed, output_weight_t, (((1,), (1,)), ((), ())), preferred_element_type=jnp.float32
    ).astype(jnp.bfloat16)
    mixer_partial, _ = lax.optimization_barrier((mixer_partial, second_full))
    mixer_total = lax.psum(mixer_partial, "head").astype(jnp.float32)
    residual = (embedded.astype(jnp.float32) + mixer_total).astype(jnp.bfloat16)
    last_residual = lax.dynamic_slice_in_dim(residual, live_count * PAGE - 1, 1, 0)
    arriving = passed_along(last_residual, "group", 1)
    channel_in = layer_norm(residual)
    channel_pages = channel_in.reshape(SLOTS, PAGE, full_width)
    edge_two = (
        jnp.concatenate([layer_norm(arriving), channel_pages[:-1, -1, :]], axis=0)
        * continues[:, None]
    )
    channel_prev = jnp.concatenate(
        [edge_two[:, None, :], channel_pages[:, :-1, :]], axis=1
    ).reshape(slot_rows, full_width)
    channel_delta = channel_prev - channel_in
    key_input = (channel_in + channel_delta * lag_blend_coefs[6]).astype(jnp.bfloat16)
    gate_input = (channel_in + channel_delta * lag_blend_coefs[7]).astype(jnp.bfloat16)
    gate_raw_two = jnp.dot(gate_input, projections[4], preferred_element_type=jnp.float32)
    key_raw = jnp.dot(key_input, key_weight, preferred_element_type=jnp.float32)
    squared = jnp.square(jax.nn.relu(key_raw)).astype(jnp.bfloat16)
    channel = lax.psum_scatter(
        lax.dot_general(
            squared, value_weight_t, (((1,), (1,)), ((), ())), preferred_element_type=jnp.float32
        ).astype(jnp.bfloat16),
        "head",
        scatter_dimension=1,
        tiled=True,
    ).astype(jnp.float32)
    gate_two = jax.nn.sigmoid(gate_raw_two)
    residual_local = lax.dynamic_slice_in_dim(
        residual, head_here * features_on_shard, features_on_shard, 1
    )
    hidden = (residual_local.astype(jnp.float32) + gate_two * channel).astype(jnp.bfloat16)
    row_live = jnp.repeat(slot_live, PAGE)
    hidden_out = jnp.where(row_live[:, None], hidden, jnp.zeros_like(hidden))
    state_out = page_end.reshape(SLOTS, attenders_on_shard, ATTENTION_DEPTH * ATTENTION_DEPTH)
    state_out = jnp.where(slot_live[:, None, None], state_out, jnp.zeros_like(state_out))
    first_edge = lax.dynamic_slice_in_dim(
        current_pages[:, -1, :], head_here * features_on_shard, features_on_shard, 1
    )
    second_edge = lax.dynamic_slice_in_dim(
        channel_pages[:, -1, :], head_here * features_on_shard, features_on_shard, 1
    )
    edge_out = jnp.stack([first_edge, second_edge], axis=1)
    edge_out = jnp.where(slot_live[:, None, None], edge_out, jnp.zeros_like(edge_out))
    return (hidden_out, state_out, edge_out)


def solution(mesh):
    in_specs = (
        P(None, "head"),
        P(None, "group", "head"),
        P("group", "head"),
        P("head", "group"),
        P("head", "group"),
        P(),
        P(),
        P(),
        P(),
        P(None, "head"),
        P("head"),
        P("head"),
        P("head"),
        P(),
        P(),
        P(),
    )
    out_specs = (P("group", "head"), P("group", "head", None), P("group", None, "head"))
    return jax.shard_map(
        per_device, mesh=mesh, in_specs=in_specs, out_specs=out_specs, check_vma=False
    )
```

```python
import jax
import jax.numpy as jnp
from jax import lax
from jax.sharding import PartitionSpec as P

ATTENTION_DEPTH = 64
PAGE = 256
SLOTS = 4
BLOCK = 128


EXACT_ARITHMETIC = lax.Precision.HIGHEST
LAYER_EPS = 1e-05
GROUP_EPS = 0.00064


def passed_along(value, axis, steps):
    count = lax.axis_size(axis)
    initial, last = (max(0, -steps), min(count, count - steps))
    return lax.ppermute(value, axis, [(source, source + steps) for source in range(initial, last)])


def layer_norm(value_rows):
    value_rows = value_rows.astype(jnp.float32)
    centered = value_rows - jnp.mean(value_rows, axis=-1, keepdims=True)
    return centered * lax.rsqrt(jnp.mean(centered * centered, axis=-1, keepdims=True) + LAYER_EPS)


def mixed_inputs(current, previous, lag_blend_coefs, blend_narrowing_map, blend_widening_maps):
    delta_rows = previous - current
    seeded = (current + delta_rows * lag_blend_coefs[0]).astype(jnp.bfloat16)
    low_rank = jnp.tanh(
        jnp.dot(seeded, blend_narrowing_map, preferred_element_type=jnp.float32)
    ).astype(jnp.bfloat16)
    rank_width = blend_widening_maps.shape[1]
    result_lines = []
    for number in range(5):
        column_part = low_rank[:, number * rank_width : (number + 1) * rank_width]
        offset = jnp.dot(
            column_part, blend_widening_maps[number], preferred_element_type=jnp.float32
        )
        result_lines.append(
            (current + delta_rows * (lag_blend_coefs[number + 1] + offset)).astype(jnp.bfloat16)
        )
    return result_lines


def log_decay(mixed_decay, fading_narrowing_map, fading_widening_map, initial_fading_power):
    hidden_low = jnp.tanh(
        jnp.dot(mixed_decay, fading_narrowing_map, preferred_element_type=jnp.float32)
    ).astype(jnp.bfloat16)
    return -jnp.exp(
        initial_fading_power
        + jnp.dot(hidden_low, fading_widening_map, preferred_element_type=jnp.float32)
    )


def group_norm(value_rows):
    shaped = value_rows.reshape(value_rows.shape[0], -1, ATTENTION_DEPTH)
    centered = shaped - jnp.mean(shaped, axis=-1, keepdims=True)
    normed = centered * lax.rsqrt(jnp.mean(centered * centered, axis=-1, keepdims=True) + GROUP_EPS)
    return normed.reshape(value_rows.shape)


def per_device(
    symbol_lookup_table,
    joined_linear_maps,
    feedforward_lookup_map,
    timeblend_result_map,
    feedforward_content_map,
    lag_blend_coefs,
    blend_narrowing_map,
    blend_widening_maps,
    fading_narrowing_map,
    fading_widening_map,
    initial_fading_power,
    present_symbol_extra,
    attender_scaling_coefs,
    active_cluster_sheets,
    sheets_for_inquiry,
    sheet_symbol_indices,
):
    group_count = lax.axis_size("group")
    group_here = lax.axis_index("group")
    head_here = lax.axis_index("head")
    features_on_shard = present_symbol_extra.shape[0]
    attenders_on_shard = features_on_shard // ATTENTION_DEPTH
    held = sheet_symbol_indices.shape[0] // group_count
    slot_rows = held * PAGE
    full_width = lag_blend_coefs.shape[1]
    group_number = jnp.arange(group_count, dtype=jnp.int32)
    pick_group = group_number == group_here
    live_count = jnp.sum(jnp.where(pick_group, active_cluster_sheets, 0))
    group_first = jnp.cumsum(active_cluster_sheets) - active_cluster_sheets
    first_page = jnp.sum(jnp.where(pick_group, group_first, 0))
    slot_number = jnp.arange(SLOTS, dtype=jnp.int32)
    slot_live = slot_number < live_count
    held_number = jnp.arange(held, dtype=jnp.int32)
    request_first = jnp.cumsum(sheets_for_inquiry) - sheets_for_inquiry
    page_here = group_here * held + held_number
    begins = jnp.any(page_here[:, None] == request_first[None, :], axis=1)
    continues = jnp.where(jnp.logical_not(begins), 1.0, 0.0).astype(jnp.float32)
    tokens_here = jnp.take(sheet_symbol_indices, page_here, axis=0)
    before_token = jnp.take(sheet_symbol_indices[:, -1], jnp.maximum(page_here - 1, 0))
    edge_pad = jnp.concatenate([before_token, jnp.zeros((8 - held,), before_token.dtype)])
    all_tokens = jnp.concatenate([tokens_here.reshape(-1), edge_pad])
    own_rows = jnp.take(symbol_lookup_table, all_tokens, axis=0)
    gathered_rows = lax.all_gather(own_rows, "head", axis=1, tiled=True)
    embedded = gathered_rows[:slot_rows]
    edge_rows = gathered_rows[slot_rows : slot_rows + held]
    map_count = joined_linear_maps.shape[0]
    first_pack = jnp.concatenate(
        [joined_linear_maps, timeblend_result_map.T[None]], axis=0
    ).astype(jnp.bfloat16)
    second_pack = jnp.stack(
        [feedforward_lookup_map, feedforward_content_map.T], axis=0
    ).astype(jnp.bfloat16)
    first_pack, _ = lax.optimization_barrier((first_pack, gathered_rows))
    first_full = lax.all_gather(first_pack, "group", axis=1, tiled=True)
    second_pack, _ = lax.optimization_barrier((second_pack, first_full))
    second_full = lax.all_gather(second_pack, "group", axis=1, tiled=True)
    projections = first_full[:map_count]
    output_weight_t = first_full[map_count]
    key_weight = second_full[0]
    value_weight_t = second_full[1]
    current = layer_norm(embedded)
    edge_first = layer_norm(edge_rows) * continues[:, None]
    current_pages = current.reshape(held, PAGE, full_width)
    previous = jnp.concatenate([edge_first[:, None, :], current_pages[:, :-1, :]], axis=1).reshape(
        slot_rows, full_width
    )
    mixed_decay, mixed_key, mixed_value, mixed_query, mixed_gate = mixed_inputs(
        current, previous, lag_blend_coefs, blend_narrowing_map, blend_widening_maps
    )
    fading_multipliers = log_decay(
        mixed_decay, fading_narrowing_map, fading_widening_map, initial_fading_power
    )
    acceptance_lines = jnp.dot(mixed_query, projections[0], preferred_element_type=jnp.float32)
    present_lookups = jnp.dot(mixed_key, projections[1], preferred_element_type=jnp.float32)
    present_contents = jnp.dot(mixed_value, projections[2], preferred_element_type=jnp.float32)
    gate_raw = jnp.dot(mixed_gate, projections[3], preferred_element_type=jnp.float32)
    gating = jax.nn.silu(gate_raw)
    blocks = slot_rows // BLOCK
    per_page = PAGE // BLOCK

    def to_blocks(value_rows):
        return value_rows.reshape(blocks, BLOCK, attenders_on_shard, ATTENTION_DEPTH).transpose(
            0, 2, 1, 3
        )

    block_index = jnp.arange(blocks, dtype=jnp.int32)
    block_start = block_index % per_page == 0
    block_slot = block_index // per_page
    slot_keep = continues * (held_number > 0)
    keep_state = jnp.where(block_start, jnp.take(slot_keep, block_slot), 1.0)
    keep_factor = jnp.where(block_start, jnp.take(continues, block_slot), 1.0)
    attender_extra = present_symbol_extra.reshape(attenders_on_shard, ATTENTION_DEPTH)
    strictly_lower = jnp.arange(BLOCK)[:, None] > jnp.arange(BLOCK)[None, :]

    askers_b = to_blocks(acceptance_lines)
    lookups_b = to_blocks(present_lookups)
    values_b = to_blocks(present_contents)
    decay_b = to_blocks(fading_multipliers)
    inclusive = jnp.cumsum(decay_b, axis=2)
    exclusive = inclusive - decay_b
    query_scaled = askers_b * jnp.exp(exclusive)
    key_scaled = lookups_b * jnp.exp(-inclusive)
    scores = jnp.einsum("bhts,bhus->bhtu", query_scaled, key_scaled, precision=EXACT_ARITHMETIC)
    scores = jnp.where(strictly_lower, scores, 0.0)
    selfpair_contribution = jnp.sum(askers_b * attender_extra[None, :, None, :] * lookups_b, axis=3)
    intra = (
        jnp.einsum("bhtu,bhuj->bhtj", scores, values_b, precision=EXACT_ARITHMETIC)
        + selfpair_contribution[..., None] * values_b
    )
    block_total = inclusive[:, :, -1, :]
    block_decay = jnp.exp(block_total)
    key_end = lookups_b * jnp.exp(block_total[:, :, None, :] - inclusive)
    block_kv = jnp.einsum("bhts,bhtj->bhsj", key_end, values_b, precision=EXACT_ARITHMETIC)
    sweep = jnp.zeros((attenders_on_shard, ATTENTION_DEPTH, ATTENTION_DEPTH), jnp.float32)
    factor = jnp.ones((attenders_on_shard, ATTENTION_DEPTH), jnp.float32)
    starts, factors_before, ends, factors_after = [], [], [], []
    for number in range(blocks):
        sweep = sweep * keep_state[number]
        factor = factor * keep_factor[number]
        starts.append(sweep)
        factors_before.append(factor)
        sweep = block_decay[number][:, :, None] * sweep + block_kv[number]
        factor = factor * block_decay[number]
        ends.append(sweep)
        factors_after.append(factor)
    block_out = intra + jnp.einsum(
        "bhts,bhsj->bhtj", query_scaled, jnp.stack(starts), precision=EXACT_ARITHMETIC
    )
    carry_rows = query_scaled * jnp.stack(factors_before)[:, :, None, :]
    block_states = jnp.stack(ends)
    block_factors = jnp.stack(factors_after)
    page_end = block_states[per_page - 1 :: per_page]
    page_factor = block_factors[per_page - 1 :: per_page]
    leaving_state = page_end[-1]
    leaving_factor = page_factor[-1]

    leaving_pack = jnp.concatenate([leaving_state, leaving_factor[:, None, :]], axis=1)
    arrivals = [passed_along(leaving_pack, "group", distance) for distance in range(1, group_count)]
    incoming = jnp.zeros_like(leaving_state)
    for arrival in reversed(arrivals):
        incoming = arrival[:, ATTENTION_DEPTH, :][:, :, None] * incoming + arrival[:, :ATTENTION_DEPTH, :]
    block_out = block_out + jnp.einsum(
        "bhts,hsj->bhtj", carry_rows, incoming, precision=EXACT_ARITHMETIC
    )
    page_end = page_end + page_factor[:, :, :, None] * incoming[None]
    attended = block_out.transpose(0, 2, 1, 3).reshape(slot_rows, features_on_shard)
    normed = (group_norm(attended) * attender_scaling_coefs * gating).astype(jnp.bfloat16)
    mixer_partial = lax.dot_general(
        normed, output_weight_t, (((1,), (1,)), ((), ())), preferred_element_type=jnp.float32
    ).astype(jnp.bfloat16)
    mixer_partial, _ = lax.optimization_barrier((mixer_partial, second_full))
    mixer_total = lax.psum(mixer_partial, "head").astype(jnp.float32)
    residual = (embedded.astype(jnp.float32) + mixer_total).astype(jnp.bfloat16)
    last_residual = residual[slot_rows - 1 : slot_rows]
    arriving = passed_along(last_residual, "group", 1)
    channel_in = layer_norm(residual)
    channel_pages = channel_in.reshape(held, PAGE, full_width)
    edge_two = (
        jnp.concatenate([layer_norm(arriving), channel_pages[:-1, -1, :]], axis=0)
        * continues[:, None]
    )
    channel_prev = jnp.concatenate(
        [edge_two[:, None, :], channel_pages[:, :-1, :]], axis=1
    ).reshape(slot_rows, full_width)
    channel_delta = channel_prev - channel_in
    key_input = (channel_in + channel_delta * lag_blend_coefs[6]).astype(jnp.bfloat16)
    gate_input = (channel_in + channel_delta * lag_blend_coefs[7]).astype(jnp.bfloat16)
    gate_raw_two = jnp.dot(gate_input, projections[4], preferred_element_type=jnp.float32)
    key_raw = jnp.dot(key_input, key_weight, preferred_element_type=jnp.float32)
    squared = jnp.square(jax.nn.relu(key_raw)).astype(jnp.bfloat16)
    channel = lax.psum_scatter(
        lax.dot_general(
            squared, value_weight_t, (((1,), (1,)), ((), ())), preferred_element_type=jnp.float32
        ).astype(jnp.bfloat16),
        "head",
        scatter_dimension=1,
        tiled=True,
    ).astype(jnp.float32)
    gate_two = jax.nn.sigmoid(gate_raw_two)
    residual_local = lax.dynamic_slice_in_dim(
        residual, head_here * features_on_shard, features_on_shard, 1
    )
    hidden = (residual_local.astype(jnp.float32) + gate_two * channel).astype(jnp.bfloat16)
    state_held = page_end.reshape(held, attenders_on_shard, ATTENTION_DEPTH * ATTENTION_DEPTH)
    first_edge = lax.dynamic_slice_in_dim(
        current_pages[:, -1, :], head_here * features_on_shard, features_on_shard, 1
    )
    second_edge = lax.dynamic_slice_in_dim(
        channel_pages[:, -1, :], head_here * features_on_shard, features_on_shard, 1
    )
    edge_held = jnp.stack([first_edge, second_edge], axis=1)
    reach = 2
    shifts = range(-reach, reach + 1)

    def from_neighbours(value):
        return jnp.concatenate(
            [value if shift == 0 else passed_along(value, "group", -shift) for shift in shifts], axis=0
        )

    hidden_near = from_neighbours(hidden.reshape(held, PAGE, features_on_shard))
    state_near = from_neighbours(state_held)
    edge_near = from_neighbours(edge_held)
    slot_page = first_page + slot_number
    source_group = slot_page // held
    source_index = (source_group - group_here + reach) * held + slot_page - source_group * held
    source_index = jnp.clip(source_index, 0, (2 * reach + 1) * held - 1)
    hidden_out = jnp.take(hidden_near, source_index, axis=0)
    hidden_out = jnp.where(slot_live[:, None, None], hidden_out, jnp.zeros_like(hidden_out))
    hidden_out = hidden_out.reshape(SLOTS * PAGE, features_on_shard)
    state_out = jnp.take(state_near, source_index, axis=0)
    state_out = jnp.where(slot_live[:, None, None], state_out, jnp.zeros_like(state_out))
    edge_out = jnp.take(edge_near, source_index, axis=0)
    edge_out = jnp.where(slot_live[:, None, None], edge_out, jnp.zeros_like(edge_out))
    return (hidden_out, state_out, edge_out)


def solution(mesh):
    in_specs = (
        P(None, "head"),
        P(None, "group", "head"),
        P("group", "head"),
        P("head", "group"),
        P("head", "group"),
        P(),
        P(),
        P(),
        P(),
        P(None, "head"),
        P("head"),
        P("head"),
        P("head"),
        P(),
        P(),
        P(),
    )
    out_specs = (P("group", "head"), P("group", "head", None), P("group", None, "head"))
    return jax.shard_map(
        per_device, mesh=mesh, in_specs=in_specs, out_specs=out_specs, check_vma=False
    )
```

```python
import jax
import jax.numpy as jnp
from jax import lax
from jax.sharding import PartitionSpec as P

ATTENTION_DEPTH = 64
PAGE = 256
SLOTS = 4
BLOCK = 128


EXACT_ARITHMETIC = lax.Precision.HIGHEST
LAYER_EPS = 1e-05
GROUP_EPS = 0.00064


def passed_along(value, axis, steps):
    count = lax.axis_size(axis)
    initial, last = (max(0, -steps), min(count, count - steps))
    return lax.ppermute(value, axis, [(source, source + steps) for source in range(initial, last)])


def _swap(value, axis, flip):
    count = lax.axis_size(axis)
    return lax.ppermute(value, axis, [(s, s ^ flip) for s in range(count)])


def _ring(value, axis, step):
    count = lax.axis_size(axis)
    pairs = []
    for s in range(count):
        z = (s // 2) % 4
        target = s - z * 2 + ((z + step) % 4) * 2
        pairs.append((s, target))
    return lax.ppermute(value, axis, pairs)


def hier_reduce_scatter(partial, axis):
    h = lax.axis_index(axis)
    rows, width = partial.shape
    W = width // 16
    core = h % 2
    z = (h // 2) % 4
    yh = h // 8
    blocks = partial.reshape(rows, 2, 4, 2, W)
    mine = jnp.where(core == 0, blocks[:, :, :, 0], blocks[:, :, :, 1])
    other = jnp.where(core == 0, blocks[:, :, :, 1], blocks[:, :, :, 0])
    acc = mine.astype(jnp.float32) + _swap(other, axis, 1).astype(jnp.float32)
    acc = acc.astype(jnp.bfloat16)
    zsel = lambda a, k: jnp.take(a, k, axis=2)
    total = zsel(acc, z).astype(jnp.float32)
    for step in (1, 2, 3):
        send = zsel(acc, (z + step) % 4)
        total = total + _ring(send, axis, step).astype(jnp.float32)
    total = total.astype(jnp.bfloat16)
    keep = jnp.where(yh == 0, total[:, 0], total[:, 1])
    give = jnp.where(yh == 0, total[:, 1], total[:, 0])
    result = keep.astype(jnp.float32) + _swap(give, axis, 8).astype(jnp.float32)
    return result


def hier_all_gather(piece, axis):
    h = lax.axis_index(axis)
    core = h % 2
    z = (h // 2) % 4
    yh = h // 8
    got = _swap(piece, axis, 8)
    pair = jnp.where(yh == 0, jnp.stack([piece, got], 1), jnp.stack([got, piece], 1))
    ring_parts = [pair] + [_ring(pair, axis, -step % 4) for step in (1, 2, 3)]
    stacked = jnp.stack(ring_parts, 2)
    by_z = jnp.take(stacked, (jnp.arange(4) - z) % 4, axis=2)
    partner = _swap(by_z, axis, 1)
    both = jnp.where(core == 0, jnp.stack([by_z, partner], 3), jnp.stack([partner, by_z], 3))
    return both.reshape(piece.shape[0], 16 * piece.shape[1])


def layer_norm(value_rows):
    value_rows = value_rows.astype(jnp.float32)
    centered = value_rows - jnp.mean(value_rows, axis=-1, keepdims=True)
    return centered * lax.rsqrt(jnp.mean(centered * centered, axis=-1, keepdims=True) + LAYER_EPS)


def mixed_inputs(current, previous, lag_blend_coefs, blend_narrowing_map, blend_widening_maps):
    delta_rows = previous - current
    seeded = (current + delta_rows * lag_blend_coefs[0]).astype(jnp.bfloat16)
    low_rank = jnp.tanh(
        jnp.dot(seeded, blend_narrowing_map, preferred_element_type=jnp.float32)
    ).astype(jnp.bfloat16)
    rank_width = blend_widening_maps.shape[1]
    result_lines = []
    for number in range(5):
        column_part = low_rank[:, number * rank_width : (number + 1) * rank_width]
        offset = jnp.dot(
            column_part, blend_widening_maps[number], preferred_element_type=jnp.float32
        )
        result_lines.append(
            (current + delta_rows * (lag_blend_coefs[number + 1] + offset)).astype(jnp.bfloat16)
        )
    return result_lines


def log_decay(mixed_decay, fading_narrowing_map, fading_widening_map, initial_fading_power):
    hidden_low = jnp.tanh(
        jnp.dot(mixed_decay, fading_narrowing_map, preferred_element_type=jnp.float32)
    ).astype(jnp.bfloat16)
    return -jnp.exp(
        initial_fading_power
        + jnp.dot(hidden_low, fading_widening_map, preferred_element_type=jnp.float32)
    )


def group_norm(value_rows):
    shaped = value_rows.reshape(value_rows.shape[0], -1, ATTENTION_DEPTH)
    centered = shaped - jnp.mean(shaped, axis=-1, keepdims=True)
    normed = centered * lax.rsqrt(jnp.mean(centered * centered, axis=-1, keepdims=True) + GROUP_EPS)
    return normed.reshape(value_rows.shape)


def per_device(
    symbol_lookup_table,
    joined_linear_maps,
    feedforward_lookup_map,
    timeblend_result_map,
    feedforward_content_map,
    lag_blend_coefs,
    blend_narrowing_map,
    blend_widening_maps,
    fading_narrowing_map,
    fading_widening_map,
    initial_fading_power,
    present_symbol_extra,
    attender_scaling_coefs,
    active_cluster_sheets,
    sheets_for_inquiry,
    sheet_symbol_indices,
):
    group_count = lax.axis_size("group")
    group_here = lax.axis_index("group")
    head_here = lax.axis_index("head")
    features_on_shard = present_symbol_extra.shape[0]
    attenders_on_shard = features_on_shard // ATTENTION_DEPTH
    held = sheet_symbol_indices.shape[0] // group_count
    slot_rows = held * PAGE
    full_width = lag_blend_coefs.shape[1]
    group_number = jnp.arange(group_count, dtype=jnp.int32)
    pick_group = group_number == group_here
    live_count = jnp.sum(jnp.where(pick_group, active_cluster_sheets, 0))
    group_first = jnp.cumsum(active_cluster_sheets) - active_cluster_sheets
    first_page = jnp.sum(jnp.where(pick_group, group_first, 0))
    slot_number = jnp.arange(SLOTS, dtype=jnp.int32)
    slot_live = slot_number < live_count
    held_number = jnp.arange(held, dtype=jnp.int32)
    request_first = jnp.cumsum(sheets_for_inquiry) - sheets_for_inquiry
    page_here = group_here * held + held_number
    begins = jnp.any(page_here[:, None] == request_first[None, :], axis=1)
    continues = jnp.where(jnp.logical_not(begins), 1.0, 0.0).astype(jnp.float32)
    tokens_here = jnp.take(sheet_symbol_indices, page_here, axis=0)
    before_token = jnp.take(sheet_symbol_indices[:, -1], jnp.maximum(page_here - 1, 0))
    edge_pad = jnp.concatenate([before_token, jnp.zeros((8 - held,), before_token.dtype)])
    all_tokens = jnp.concatenate([tokens_here.reshape(-1), edge_pad])
    own_rows = jnp.take(symbol_lookup_table, all_tokens, axis=0)
    gathered_rows = lax.all_gather(own_rows, "head", axis=1, tiled=True)
    embedded = gathered_rows[:slot_rows]
    edge_rows = gathered_rows[slot_rows : slot_rows + held]
    map_count = joined_linear_maps.shape[0]
    first_pack = jnp.concatenate(
        [joined_linear_maps, timeblend_result_map.T[None]], axis=0
    ).astype(jnp.bfloat16)
    second_pack = jnp.stack(
        [feedforward_lookup_map, feedforward_content_map.T], axis=0
    ).astype(jnp.bfloat16)
    first_pack, _ = lax.optimization_barrier((first_pack, gathered_rows))
    first_full = lax.all_gather(first_pack, "group", axis=1, tiled=True)
    second_pack, _ = lax.optimization_barrier((second_pack, first_full))
    second_full = lax.all_gather(second_pack, "group", axis=1, tiled=True)
    projections = first_full[:map_count]
    output_weight_t = first_full[map_count]
    key_weight = second_full[0]
    value_weight_t = second_full[1]
    current = layer_norm(embedded)
    edge_first = layer_norm(edge_rows) * continues[:, None]
    current_pages = current.reshape(held, PAGE, full_width)
    previous = jnp.concatenate([edge_first[:, None, :], current_pages[:, :-1, :]], axis=1).reshape(
        slot_rows, full_width
    )
    mixed_decay, mixed_key, mixed_value, mixed_query, mixed_gate = mixed_inputs(
        current, previous, lag_blend_coefs, blend_narrowing_map, blend_widening_maps
    )
    fading_multipliers = log_decay(
        mixed_decay, fading_narrowing_map, fading_widening_map, initial_fading_power
    )
    acceptance_lines = jnp.dot(mixed_query, projections[0], preferred_element_type=jnp.float32)
    present_lookups = jnp.dot(mixed_key, projections[1], preferred_element_type=jnp.float32)
    present_contents = jnp.dot(mixed_value, projections[2], preferred_element_type=jnp.float32)
    gate_raw = jnp.dot(mixed_gate, projections[3], preferred_element_type=jnp.float32)
    gating = jax.nn.silu(gate_raw)
    blocks = slot_rows // BLOCK
    per_page = PAGE // BLOCK

    def to_blocks(value_rows):
        return value_rows.reshape(blocks, BLOCK, attenders_on_shard, ATTENTION_DEPTH).transpose(
            0, 2, 1, 3
        )

    block_index = jnp.arange(blocks, dtype=jnp.int32)
    block_start = block_index % per_page == 0
    block_slot = block_index // per_page
    slot_keep = continues * (held_number > 0)
    keep_state = jnp.where(block_start, jnp.take(slot_keep, block_slot), 1.0)
    keep_factor = jnp.where(block_start, jnp.take(continues, block_slot), 1.0)
    attender_extra = present_symbol_extra.reshape(attenders_on_shard, ATTENTION_DEPTH)
    strictly_lower = jnp.arange(BLOCK)[:, None] > jnp.arange(BLOCK)[None, :]

    askers_b = to_blocks(acceptance_lines)
    lookups_b = to_blocks(present_lookups)
    values_b = to_blocks(present_contents)
    decay_b = to_blocks(fading_multipliers)
    inclusive = jnp.cumsum(decay_b, axis=2)
    exclusive = inclusive - decay_b
    query_scaled = askers_b * jnp.exp(exclusive)
    key_scaled = lookups_b * jnp.exp(-inclusive)
    scores = jnp.einsum("bhts,bhus->bhtu", query_scaled, key_scaled, precision=EXACT_ARITHMETIC)
    scores = jnp.where(strictly_lower, scores, 0.0)
    selfpair_contribution = jnp.sum(askers_b * attender_extra[None, :, None, :] * lookups_b, axis=3)
    intra = (
        jnp.einsum("bhtu,bhuj->bhtj", scores, values_b, precision=EXACT_ARITHMETIC)
        + selfpair_contribution[..., None] * values_b
    )
    block_total = inclusive[:, :, -1, :]
    block_decay = jnp.exp(block_total)
    key_end = lookups_b * jnp.exp(block_total[:, :, None, :] - inclusive)
    block_kv = jnp.einsum("bhts,bhtj->bhsj", key_end, values_b, precision=EXACT_ARITHMETIC)
    sweep = jnp.zeros((attenders_on_shard, ATTENTION_DEPTH, ATTENTION_DEPTH), jnp.float32)
    factor = jnp.ones((attenders_on_shard, ATTENTION_DEPTH), jnp.float32)
    starts, factors_before, ends, factors_after = [], [], [], []
    for number in range(blocks):
        sweep = sweep * keep_state[number]
        factor = factor * keep_factor[number]
        starts.append(sweep)
        factors_before.append(factor)
        sweep = block_decay[number][:, :, None] * sweep + block_kv[number]
        factor = factor * block_decay[number]
        ends.append(sweep)
        factors_after.append(factor)
    block_out = intra + jnp.einsum(
        "bhts,bhsj->bhtj", query_scaled, jnp.stack(starts), precision=EXACT_ARITHMETIC
    )
    carry_rows = query_scaled * jnp.stack(factors_before)[:, :, None, :]
    block_states = jnp.stack(ends)
    block_factors = jnp.stack(factors_after)
    page_end = block_states[per_page - 1 :: per_page]
    page_factor = block_factors[per_page - 1 :: per_page]
    leaving_state = page_end[-1]
    leaving_factor = page_factor[-1]

    leaving_pack = jnp.concatenate([leaving_state, leaving_factor[:, None, :]], axis=1)
    arrivals = [passed_along(leaving_pack, "group", distance) for distance in range(1, group_count)]
    incoming = jnp.zeros_like(leaving_state)
    for arrival in reversed(arrivals):
        incoming = arrival[:, ATTENTION_DEPTH, :][:, :, None] * incoming + arrival[:, :ATTENTION_DEPTH, :]
    block_out = block_out + jnp.einsum(
        "bhts,hsj->bhtj", carry_rows, incoming, precision=EXACT_ARITHMETIC
    )
    page_end = page_end + page_factor[:, :, :, None] * incoming[None]
    attended = block_out.transpose(0, 2, 1, 3).reshape(slot_rows, features_on_shard)
    normed = (group_norm(attended) * attender_scaling_coefs * gating).astype(jnp.bfloat16)
    mixer_partial = lax.dot_general(
        normed, output_weight_t, (((1,), (1,)), ((), ())), preferred_element_type=jnp.float32
    ).astype(jnp.bfloat16)
    mixer_owned = hier_reduce_scatter(mixer_partial, "head").astype(jnp.bfloat16)
    mixer_total = hier_all_gather(mixer_owned, "head").astype(jnp.float32)
    residual = (embedded.astype(jnp.float32) + mixer_total).astype(jnp.bfloat16)
    last_residual = residual[slot_rows - 1 : slot_rows]
    arriving = passed_along(last_residual, "group", 1)
    channel_in = layer_norm(residual)
    channel_pages = channel_in.reshape(held, PAGE, full_width)
    edge_two = (
        jnp.concatenate([layer_norm(arriving), channel_pages[:-1, -1, :]], axis=0)
        * continues[:, None]
    )
    channel_prev = jnp.concatenate(
        [edge_two[:, None, :], channel_pages[:, :-1, :]], axis=1
    ).reshape(slot_rows, full_width)
    channel_delta = channel_prev - channel_in
    key_input = (channel_in + channel_delta * lag_blend_coefs[6]).astype(jnp.bfloat16)
    gate_input = (channel_in + channel_delta * lag_blend_coefs[7]).astype(jnp.bfloat16)
    gate_raw_two = jnp.dot(gate_input, projections[4], preferred_element_type=jnp.float32)
    key_raw = jnp.dot(key_input, key_weight, preferred_element_type=jnp.float32)
    squared = jnp.square(jax.nn.relu(key_raw)).astype(jnp.bfloat16)
    channel = hier_reduce_scatter(
        lax.dot_general(
            squared, value_weight_t, (((1,), (1,)), ((), ())), preferred_element_type=jnp.float32
        ).astype(jnp.bfloat16),
        "head",
    )
    gate_two = jax.nn.sigmoid(gate_raw_two)
    residual_local = lax.dynamic_slice_in_dim(
        residual, head_here * features_on_shard, features_on_shard, 1
    )
    hidden = (residual_local.astype(jnp.float32) + gate_two * channel).astype(jnp.bfloat16)
    state_held = page_end.reshape(held, attenders_on_shard, ATTENTION_DEPTH * ATTENTION_DEPTH)
    first_edge = lax.dynamic_slice_in_dim(
        current_pages[:, -1, :], head_here * features_on_shard, features_on_shard, 1
    )
    second_edge = lax.dynamic_slice_in_dim(
        channel_pages[:, -1, :], head_here * features_on_shard, features_on_shard, 1
    )
    edge_held = jnp.stack([first_edge, second_edge], axis=1)
    reach = 2
    shifts = range(-reach, reach + 1)

    def from_neighbours(value):
        return jnp.concatenate(
            [value if shift == 0 else passed_along(value, "group", -shift) for shift in shifts], axis=0
        )

    hidden_near = from_neighbours(hidden.reshape(held, PAGE, features_on_shard))
    state_near = from_neighbours(state_held)
    edge_near = from_neighbours(edge_held)
    slot_page = first_page + slot_number
    source_group = slot_page // held
    source_index = (source_group - group_here + reach) * held + slot_page - source_group * held
    source_index = jnp.clip(source_index, 0, (2 * reach + 1) * held - 1)
    hidden_out = jnp.take(hidden_near, source_index, axis=0)
    hidden_out = jnp.where(slot_live[:, None, None], hidden_out, jnp.zeros_like(hidden_out))
    hidden_out = hidden_out.reshape(SLOTS * PAGE, features_on_shard)
    state_out = jnp.take(state_near, source_index, axis=0)
    state_out = jnp.where(slot_live[:, None, None], state_out, jnp.zeros_like(state_out))
    edge_out = jnp.take(edge_near, source_index, axis=0)
    edge_out = jnp.where(slot_live[:, None, None], edge_out, jnp.zeros_like(edge_out))
    return (hidden_out, state_out, edge_out)


def solution(mesh):
    in_specs = (
        P(None, "head"),
        P(None, "group", "head"),
        P("group", "head"),
        P("head", "group"),
        P("head", "group"),
        P(),
        P(),
        P(),
        P(),
        P(None, "head"),
        P("head"),
        P("head"),
        P("head"),
        P(),
        P(),
        P(),
    )
    out_specs = (P("group", "head"), P("group", "head", None), P("group", None, "head"))
    return jax.shard_map(
        per_device, mesh=mesh, in_specs=in_specs, out_specs=out_specs, check_vma=False
    )
```

```python
import jax
import jax.numpy as jnp
from jax import lax
from jax.sharding import PartitionSpec as P

ATTENTION_DEPTH = 64
PAGE = 256
SLOTS = 4
BLOCK = 128


EXACT_ARITHMETIC = lax.Precision.HIGHEST
LAYER_EPS = 1e-05
GROUP_EPS = 0.00064


def passed_along(value, axis, steps):
    count = lax.axis_size(axis)
    initial, last = (max(0, -steps), min(count, count - steps))
    return lax.ppermute(value, axis, [(source, source + steps) for source in range(initial, last)])


def _swap(value, axis, flip):
    count = lax.axis_size(axis)
    return lax.ppermute(value, axis, [(s, s ^ flip) for s in range(count)])


def _ring(value, axis, step):
    count = lax.axis_size(axis)
    pairs = []
    for s in range(count):
        z = (s // 2) % 4
        target = s - z * 2 + ((z + step) % 4) * 2
        pairs.append((s, target))
    return lax.ppermute(value, axis, pairs)


def hier_reduce_scatter(partial, axis):
    h = lax.axis_index(axis)
    rows, width = partial.shape
    W = width // 16
    core = h % 2
    z = (h // 2) % 4
    yh = h // 8
    blocks = partial.reshape(rows, 2, 4, 2, W)
    mine = jnp.where(core == 0, blocks[:, :, :, 0], blocks[:, :, :, 1])
    other = jnp.where(core == 0, blocks[:, :, :, 1], blocks[:, :, :, 0])
    acc = mine.astype(jnp.float32) + _swap(other, axis, 1).astype(jnp.float32)
    acc = acc.astype(jnp.bfloat16)
    zsel = lambda a, k: jnp.take(a, k, axis=2)
    total = zsel(acc, z).astype(jnp.float32)
    for step in (1, 2, 3):
        send = zsel(acc, (z + step) % 4)
        total = total + _ring(send, axis, step).astype(jnp.float32)
    total = total.astype(jnp.bfloat16)
    keep = jnp.where(yh == 0, total[:, 0], total[:, 1])
    give = jnp.where(yh == 0, total[:, 1], total[:, 0])
    result = keep.astype(jnp.float32) + _swap(give, axis, 8).astype(jnp.float32)
    return result


def hier_all_gather(piece, axis):
    h = lax.axis_index(axis)
    core = h % 2
    z = (h // 2) % 4
    yh = h // 8
    got = _swap(piece, axis, 8)
    pair = jnp.where(yh == 0, jnp.stack([piece, got], 1), jnp.stack([got, piece], 1))
    ring_parts = [pair] + [_ring(pair, axis, -step % 4) for step in (1, 2, 3)]
    stacked = jnp.stack(ring_parts, 2)
    by_z = jnp.take(stacked, (jnp.arange(4) - z) % 4, axis=2)
    partner = _swap(by_z, axis, 1)
    both = jnp.where(core == 0, jnp.stack([by_z, partner], 3), jnp.stack([partner, by_z], 3))
    return both.reshape(piece.shape[0], 16 * piece.shape[1])


def layer_norm(value_rows):
    value_rows = value_rows.astype(jnp.float32)
    centered = value_rows - jnp.mean(value_rows, axis=-1, keepdims=True)
    return centered * lax.rsqrt(jnp.mean(centered * centered, axis=-1, keepdims=True) + LAYER_EPS)


def mixed_inputs(current, previous, lag_blend_coefs, blend_narrowing_map, blend_widening_maps):
    delta_rows = previous - current
    seeded = (current + delta_rows * lag_blend_coefs[0]).astype(jnp.bfloat16)
    low_rank = jnp.tanh(
        jnp.dot(seeded, blend_narrowing_map, preferred_element_type=jnp.float32)
    ).astype(jnp.bfloat16)
    rank_width = blend_widening_maps.shape[1]
    result_lines = []
    for number in range(5):
        column_part = low_rank[:, number * rank_width : (number + 1) * rank_width]
        offset = jnp.dot(
            column_part, blend_widening_maps[number], preferred_element_type=jnp.float32
        )
        result_lines.append(
            (current + delta_rows * (lag_blend_coefs[number + 1] + offset)).astype(jnp.bfloat16)
        )
    return result_lines


def log_decay(mixed_decay, fading_narrowing_map, fading_widening_map, initial_fading_power):
    hidden_low = jnp.tanh(
        jnp.dot(mixed_decay, fading_narrowing_map, preferred_element_type=jnp.float32)
    ).astype(jnp.bfloat16)
    return -jnp.exp(
        initial_fading_power
        + jnp.dot(hidden_low, fading_widening_map, preferred_element_type=jnp.float32)
    )


def group_norm(value_rows):
    shaped = value_rows.reshape(value_rows.shape[0], -1, ATTENTION_DEPTH)
    centered = shaped - jnp.mean(shaped, axis=-1, keepdims=True)
    normed = centered * lax.rsqrt(jnp.mean(centered * centered, axis=-1, keepdims=True) + GROUP_EPS)
    return normed.reshape(value_rows.shape)


def per_device(
    symbol_lookup_table,
    joined_linear_maps,
    feedforward_lookup_map,
    timeblend_result_map,
    feedforward_content_map,
    lag_blend_coefs,
    blend_narrowing_map,
    blend_widening_maps,
    fading_narrowing_map,
    fading_widening_map,
    initial_fading_power,
    present_symbol_extra,
    attender_scaling_coefs,
    active_cluster_sheets,
    sheets_for_inquiry,
    sheet_symbol_indices,
):
    group_count = lax.axis_size("group")
    group_here = lax.axis_index("group")
    head_here = lax.axis_index("head")
    features_on_shard = present_symbol_extra.shape[0]
    attenders_on_shard = features_on_shard // ATTENTION_DEPTH
    held = sheet_symbol_indices.shape[0] // group_count
    slot_rows = held * PAGE
    full_width = lag_blend_coefs.shape[1]
    group_number = jnp.arange(group_count, dtype=jnp.int32)
    pick_group = group_number == group_here
    live_count = jnp.sum(jnp.where(pick_group, active_cluster_sheets, 0))
    group_first = jnp.cumsum(active_cluster_sheets) - active_cluster_sheets
    first_page = jnp.sum(jnp.where(pick_group, group_first, 0))
    slot_number = jnp.arange(SLOTS, dtype=jnp.int32)
    slot_live = slot_number < live_count
    held_number = jnp.arange(held, dtype=jnp.int32)
    request_first = jnp.cumsum(sheets_for_inquiry) - sheets_for_inquiry
    page_here = group_here * held + held_number
    begins = jnp.any(page_here[:, None] == request_first[None, :], axis=1)
    continues = jnp.where(jnp.logical_not(begins), 1.0, 0.0).astype(jnp.float32)
    tokens_here = jnp.take(sheet_symbol_indices, page_here, axis=0)
    before_token = jnp.take(sheet_symbol_indices[:, -1], jnp.maximum(page_here - 1, 0))
    edge_pad = jnp.concatenate([before_token, jnp.zeros((8 - held,), before_token.dtype)])
    all_tokens = jnp.concatenate([tokens_here.reshape(-1), edge_pad])
    own_rows = jnp.take(symbol_lookup_table, all_tokens, axis=0)
    gathered_rows = lax.all_gather(own_rows, "head", axis=1, tiled=True)
    embedded = gathered_rows[:slot_rows]
    edge_rows = gathered_rows[slot_rows : slot_rows + held]
    first_pack = joined_linear_maps.astype(jnp.bfloat16)
    second_pack = jnp.stack(
        [feedforward_lookup_map, feedforward_content_map.T], axis=0
    ).astype(jnp.bfloat16)
    first_pack, _ = lax.optimization_barrier((first_pack, gathered_rows))
    first_full = lax.all_gather(first_pack, "group", axis=1, tiled=True)
    output_pack, _ = lax.optimization_barrier((timeblend_result_map.astype(jnp.bfloat16), first_full))
    output_pieces = lax.all_gather(output_pack, ("group", "head"), axis=0, tiled=False)
    output_rows, output_cols = timeblend_result_map.shape
    output_weight = (
        output_pieces.reshape(group_count, -1, output_rows, output_cols)
        .transpose(1, 2, 0, 3)
        .reshape(-1, group_count * output_cols)
    )
    second_pack, _ = lax.optimization_barrier((second_pack, output_pieces))
    second_full = lax.all_gather(second_pack, "group", axis=1, tiled=True)
    projections = first_full
    key_weight = second_full[0]
    value_weight_t = second_full[1]
    current = layer_norm(embedded)
    edge_first = layer_norm(edge_rows) * continues[:, None]
    current_pages = current.reshape(held, PAGE, full_width)
    previous = jnp.concatenate([edge_first[:, None, :], current_pages[:, :-1, :]], axis=1).reshape(
        slot_rows, full_width
    )
    mixed_decay, mixed_key, mixed_value, mixed_query, mixed_gate = mixed_inputs(
        current, previous, lag_blend_coefs, blend_narrowing_map, blend_widening_maps
    )
    fading_multipliers = log_decay(
        mixed_decay, fading_narrowing_map, fading_widening_map, initial_fading_power
    )
    acceptance_lines = jnp.dot(mixed_query, projections[0], preferred_element_type=jnp.float32)
    present_lookups = jnp.dot(mixed_key, projections[1], preferred_element_type=jnp.float32)
    present_contents = jnp.dot(mixed_value, projections[2], preferred_element_type=jnp.float32)
    gate_raw = jnp.dot(mixed_gate, projections[3], preferred_element_type=jnp.float32)
    gating = jax.nn.silu(gate_raw)
    blocks = slot_rows // BLOCK
    per_page = PAGE // BLOCK

    def to_blocks(value_rows):
        return value_rows.reshape(blocks, BLOCK, attenders_on_shard, ATTENTION_DEPTH).transpose(
            0, 2, 1, 3
        )

    block_index = jnp.arange(blocks, dtype=jnp.int32)
    block_start = block_index % per_page == 0
    block_slot = block_index // per_page
    slot_keep = continues * (held_number > 0)
    keep_state = jnp.where(block_start, jnp.take(slot_keep, block_slot), 1.0)
    keep_factor = jnp.where(block_start, jnp.take(continues, block_slot), 1.0)
    attender_extra = present_symbol_extra.reshape(attenders_on_shard, ATTENTION_DEPTH)
    strictly_lower = jnp.arange(BLOCK)[:, None] > jnp.arange(BLOCK)[None, :]

    askers_b = to_blocks(acceptance_lines)
    lookups_b = to_blocks(present_lookups)
    values_b = to_blocks(present_contents)
    decay_b = to_blocks(fading_multipliers)
    inclusive = jnp.cumsum(decay_b, axis=2)
    exclusive = inclusive - decay_b
    query_scaled = askers_b * jnp.exp(exclusive)
    key_scaled = lookups_b * jnp.exp(-inclusive)
    scores = jnp.einsum("bhts,bhus->bhtu", query_scaled, key_scaled, precision=EXACT_ARITHMETIC)
    scores = jnp.where(strictly_lower, scores, 0.0)
    selfpair_contribution = jnp.sum(askers_b * attender_extra[None, :, None, :] * lookups_b, axis=3)
    intra = (
        jnp.einsum("bhtu,bhuj->bhtj", scores, values_b, precision=EXACT_ARITHMETIC)
        + selfpair_contribution[..., None] * values_b
    )
    block_total = inclusive[:, :, -1, :]
    block_decay = jnp.exp(block_total)
    key_end = lookups_b * jnp.exp(block_total[:, :, None, :] - inclusive)
    block_kv = jnp.einsum("bhts,bhtj->bhsj", key_end, values_b, precision=EXACT_ARITHMETIC)
    sweep = jnp.zeros((attenders_on_shard, ATTENTION_DEPTH, ATTENTION_DEPTH), jnp.float32)
    factor = jnp.ones((attenders_on_shard, ATTENTION_DEPTH), jnp.float32)
    starts, factors_before, ends, factors_after = [], [], [], []
    for number in range(blocks):
        sweep = sweep * keep_state[number]
        factor = factor * keep_factor[number]
        starts.append(sweep)
        factors_before.append(factor)
        sweep = block_decay[number][:, :, None] * sweep + block_kv[number]
        factor = factor * block_decay[number]
        ends.append(sweep)
        factors_after.append(factor)
    block_out = intra + jnp.einsum(
        "bhts,bhsj->bhtj", query_scaled, jnp.stack(starts), precision=EXACT_ARITHMETIC
    )
    carry_rows = query_scaled * jnp.stack(factors_before)[:, :, None, :]
    block_states = jnp.stack(ends)
    block_factors = jnp.stack(factors_after)
    page_end = block_states[per_page - 1 :: per_page]
    page_factor = block_factors[per_page - 1 :: per_page]
    leaving_state = page_end[-1]
    leaving_factor = page_factor[-1]

    leaving_pack = jnp.concatenate([leaving_state, leaving_factor[:, None, :]], axis=1)
    arrivals = [passed_along(leaving_pack, "group", distance) for distance in range(1, group_count)]
    incoming = jnp.zeros_like(leaving_state)
    for arrival in reversed(arrivals):
        incoming = arrival[:, ATTENTION_DEPTH, :][:, :, None] * incoming + arrival[:, :ATTENTION_DEPTH, :]
    block_out = block_out + jnp.einsum(
        "bhts,hsj->bhtj", carry_rows, incoming, precision=EXACT_ARITHMETIC
    )
    page_end = page_end + page_factor[:, :, :, None] * incoming[None]
    attended = block_out.transpose(0, 2, 1, 3).reshape(slot_rows, features_on_shard)
    normed = (group_norm(attended) * attender_scaling_coefs * gating).astype(jnp.bfloat16)
    normed_full = hier_all_gather(normed, "head")
    mixer_total = jnp.dot(normed_full, output_weight, preferred_element_type=jnp.float32)
    residual = (embedded.astype(jnp.float32) + mixer_total).astype(jnp.bfloat16)
    last_residual = residual[slot_rows - 1 : slot_rows]
    arriving = passed_along(last_residual, "group", 1)
    channel_in = layer_norm(residual)
    channel_pages = channel_in.reshape(held, PAGE, full_width)
    edge_two = (
        jnp.concatenate([layer_norm(arriving), channel_pages[:-1, -1, :]], axis=0)
        * continues[:, None]
    )
    channel_prev = jnp.concatenate(
        [edge_two[:, None, :], channel_pages[:, :-1, :]], axis=1
    ).reshape(slot_rows, full_width)
    channel_delta = channel_prev - channel_in
    key_input = (channel_in + channel_delta * lag_blend_coefs[6]).astype(jnp.bfloat16)
    gate_input = (channel_in + channel_delta * lag_blend_coefs[7]).astype(jnp.bfloat16)
    gate_raw_two = jnp.dot(gate_input, projections[4], preferred_element_type=jnp.float32)
    key_raw = jnp.dot(key_input, key_weight, preferred_element_type=jnp.float32)
    squared = jnp.square(jax.nn.relu(key_raw)).astype(jnp.bfloat16)
    channel = hier_reduce_scatter(
        lax.dot_general(
            squared, value_weight_t, (((1,), (1,)), ((), ())), preferred_element_type=jnp.float32
        ).astype(jnp.bfloat16),
        "head",
    )
    gate_two = jax.nn.sigmoid(gate_raw_two)
    residual_local = lax.dynamic_slice_in_dim(
        residual, head_here * features_on_shard, features_on_shard, 1
    )
    hidden = (residual_local.astype(jnp.float32) + gate_two * channel).astype(jnp.bfloat16)
    state_held = page_end.reshape(held, attenders_on_shard, ATTENTION_DEPTH * ATTENTION_DEPTH)
    first_edge = lax.dynamic_slice_in_dim(
        current_pages[:, -1, :], head_here * features_on_shard, features_on_shard, 1
    )
    second_edge = lax.dynamic_slice_in_dim(
        channel_pages[:, -1, :], head_here * features_on_shard, features_on_shard, 1
    )
    edge_held = jnp.stack([first_edge, second_edge], axis=1)
    reach = 2
    shifts = range(-reach, reach + 1)

    def from_neighbours(value):
        return jnp.concatenate(
            [value if shift == 0 else passed_along(value, "group", -shift) for shift in shifts], axis=0
        )

    hidden_near = from_neighbours(hidden.reshape(held, PAGE, features_on_shard))
    state_near = from_neighbours(state_held)
    edge_near = from_neighbours(edge_held)
    slot_page = first_page + slot_number
    source_group = slot_page // held
    source_index = (source_group - group_here + reach) * held + slot_page - source_group * held
    source_index = jnp.clip(source_index, 0, (2 * reach + 1) * held - 1)
    hidden_out = jnp.take(hidden_near, source_index, axis=0)
    hidden_out = jnp.where(slot_live[:, None, None], hidden_out, jnp.zeros_like(hidden_out))
    hidden_out = hidden_out.reshape(SLOTS * PAGE, features_on_shard)
    state_out = jnp.take(state_near, source_index, axis=0)
    state_out = jnp.where(slot_live[:, None, None], state_out, jnp.zeros_like(state_out))
    edge_out = jnp.take(edge_near, source_index, axis=0)
    edge_out = jnp.where(slot_live[:, None, None], edge_out, jnp.zeros_like(edge_out))
    return (hidden_out, state_out, edge_out)


def solution(mesh):
    in_specs = (
        P(None, "head"),
        P(None, "group", "head"),
        P("group", "head"),
        P("head", "group"),
        P("head", "group"),
        P(),
        P(),
        P(),
        P(),
        P(None, "head"),
        P("head"),
        P("head"),
        P("head"),
        P(),
        P(),
        P(),
    )
    out_specs = (P("group", "head"), P("group", "head", None), P("group", None, "head"))
    return jax.shard_map(
        per_device, mesh=mesh, in_specs=in_specs, out_specs=out_specs, check_vma=False
    )
```

```python
import jax
import jax.numpy as jnp
from jax import lax
from jax.sharding import PartitionSpec as P

ATTENTION_DEPTH = 64
PAGE = 256
SLOTS = 4
BLOCK = 128


EXACT_ARITHMETIC = lax.Precision.HIGHEST
LAYER_EPS = 1e-05
GROUP_EPS = 0.00064


def passed_along(value, axis, steps):
    count = lax.axis_size(axis)
    initial, last = (max(0, -steps), min(count, count - steps))
    return lax.ppermute(value, axis, [(source, source + steps) for source in range(initial, last)])


def _swap(value, axis, flip):
    count = lax.axis_size(axis)
    return lax.ppermute(value, axis, [(s, s ^ flip) for s in range(count)])


def _ring(value, axis, step):
    count = lax.axis_size(axis)
    pairs = []
    for s in range(count):
        z = (s // 2) % 4
        target = s - z * 2 + ((z + step) % 4) * 2
        pairs.append((s, target))
    return lax.ppermute(value, axis, pairs)


def hier_reduce_scatter(partial, axis):
    h = lax.axis_index(axis)
    rows, width = partial.shape
    W = width // 16
    core = h % 2
    z = (h // 2) % 4
    yh = h // 8
    blocks = partial.reshape(rows, 2, 4, 2, W)
    mine = jnp.where(core == 0, blocks[:, :, :, 0], blocks[:, :, :, 1])
    other = jnp.where(core == 0, blocks[:, :, :, 1], blocks[:, :, :, 0])
    acc = mine.astype(jnp.float32) + _swap(other, axis, 1).astype(jnp.float32)
    acc = acc.astype(jnp.bfloat16)
    zsel = lambda a, k: jnp.take(a, k, axis=2)
    total = zsel(acc, z).astype(jnp.float32)
    for step in (1, 2, 3):
        send = zsel(acc, (z + step) % 4)
        total = total + _ring(send, axis, step).astype(jnp.float32)
    total = total.astype(jnp.bfloat16)
    keep = jnp.where(yh == 0, total[:, 0], total[:, 1])
    give = jnp.where(yh == 0, total[:, 1], total[:, 0])
    result = keep.astype(jnp.float32) + _swap(give, axis, 8).astype(jnp.float32)
    return result


def hier_all_gather(piece, axis):
    h = lax.axis_index(axis)
    core = h % 2
    z = (h // 2) % 4
    yh = h // 8
    got = _swap(piece, axis, 8)
    pair = jnp.where(yh == 0, jnp.stack([piece, got], 1), jnp.stack([got, piece], 1))
    ring_parts = [pair] + [_ring(pair, axis, -step % 4) for step in (1, 2, 3)]
    stacked = jnp.stack(ring_parts, 2)
    by_z = jnp.take(stacked, (jnp.arange(4) - z) % 4, axis=2)
    partner = _swap(by_z, axis, 1)
    both = jnp.where(core == 0, jnp.stack([by_z, partner], 3), jnp.stack([partner, by_z], 3))
    return both.reshape(piece.shape[0], 16 * piece.shape[1])


def layer_norm(value_rows):
    value_rows = value_rows.astype(jnp.float32)
    centered = value_rows - jnp.mean(value_rows, axis=-1, keepdims=True)
    return centered * lax.rsqrt(jnp.mean(centered * centered, axis=-1, keepdims=True) + LAYER_EPS)


def mixed_inputs(current, previous, lag_blend_coefs, blend_narrowing_map, blend_widening_maps):
    delta_rows = previous - current
    seeded = (current + delta_rows * lag_blend_coefs[0]).astype(jnp.bfloat16)
    low_rank = jnp.tanh(
        jnp.dot(seeded, blend_narrowing_map, preferred_element_type=jnp.float32)
    ).astype(jnp.bfloat16)
    rank_width = blend_widening_maps.shape[1]
    result_lines = []
    for number in range(5):
        column_part = low_rank[:, number * rank_width : (number + 1) * rank_width]
        offset = jnp.dot(
            column_part, blend_widening_maps[number], preferred_element_type=jnp.float32
        )
        result_lines.append(
            (current + delta_rows * (lag_blend_coefs[number + 1] + offset)).astype(jnp.bfloat16)
        )
    return result_lines


def log_decay(mixed_decay, fading_narrowing_map, fading_widening_map, initial_fading_power):
    hidden_low = jnp.tanh(
        jnp.dot(mixed_decay, fading_narrowing_map, preferred_element_type=jnp.float32)
    ).astype(jnp.bfloat16)
    return -jnp.exp(
        initial_fading_power
        + jnp.dot(hidden_low, fading_widening_map, preferred_element_type=jnp.float32)
    )


def group_norm(value_rows):
    shaped = value_rows.reshape(value_rows.shape[0], -1, ATTENTION_DEPTH)
    centered = shaped - jnp.mean(shaped, axis=-1, keepdims=True)
    normed = centered * lax.rsqrt(jnp.mean(centered * centered, axis=-1, keepdims=True) + GROUP_EPS)
    return normed.reshape(value_rows.shape)


def per_device(
    symbol_lookup_table,
    joined_linear_maps,
    feedforward_lookup_map,
    timeblend_result_map,
    feedforward_content_map,
    lag_blend_coefs,
    blend_narrowing_map,
    blend_widening_maps,
    fading_narrowing_map,
    fading_widening_map,
    initial_fading_power,
    present_symbol_extra,
    attender_scaling_coefs,
    active_cluster_sheets,
    sheets_for_inquiry,
    sheet_symbol_indices,
):
    group_count = lax.axis_size("group")
    group_here = lax.axis_index("group")
    head_here = lax.axis_index("head")
    features_on_shard = present_symbol_extra.shape[0]
    attenders_on_shard = features_on_shard // ATTENTION_DEPTH
    held = sheet_symbol_indices.shape[0] // group_count
    slot_rows = held * PAGE
    full_width = lag_blend_coefs.shape[1]
    group_number = jnp.arange(group_count, dtype=jnp.int32)
    pick_group = group_number == group_here
    live_count = jnp.sum(jnp.where(pick_group, active_cluster_sheets, 0))
    group_first = jnp.cumsum(active_cluster_sheets) - active_cluster_sheets
    first_page = jnp.sum(jnp.where(pick_group, group_first, 0))
    slot_number = jnp.arange(SLOTS, dtype=jnp.int32)
    slot_live = slot_number < live_count
    held_number = jnp.arange(held, dtype=jnp.int32)
    request_first = jnp.cumsum(sheets_for_inquiry) - sheets_for_inquiry
    page_here = group_here * held + held_number
    begins = jnp.any(page_here[:, None] == request_first[None, :], axis=1)
    continues = jnp.where(jnp.logical_not(begins), 1.0, 0.0).astype(jnp.float32)
    tokens_here = jnp.take(sheet_symbol_indices, page_here, axis=0)
    before_token = jnp.take(sheet_symbol_indices[:, -1], jnp.maximum(page_here - 1, 0))
    edge_pad = jnp.concatenate([before_token, jnp.zeros((8 - held,), before_token.dtype)])
    all_tokens = jnp.concatenate([tokens_here.reshape(-1), edge_pad])
    own_rows = jnp.take(symbol_lookup_table, all_tokens, axis=0)
    gathered_rows = hier_all_gather(own_rows, "head")
    embedded = gathered_rows[:slot_rows]
    edge_rows = gathered_rows[slot_rows : slot_rows + held]
    map_count = joined_linear_maps.shape[0]
    first_pack = jnp.concatenate(
        [joined_linear_maps, timeblend_result_map.T[None]], axis=0
    ).astype(jnp.bfloat16)
    second_pack = jnp.stack(
        [feedforward_lookup_map, feedforward_content_map.T], axis=0
    ).astype(jnp.bfloat16)
    first_pack, _ = lax.optimization_barrier((first_pack, gathered_rows))
    first_full = lax.all_gather(first_pack, "group", axis=1, tiled=True)
    second_pack, _ = lax.optimization_barrier((second_pack, first_full))
    second_full = lax.all_gather(second_pack, "group", axis=1, tiled=True)
    projections = first_full[:map_count]
    output_weight_t = first_full[map_count]
    key_weight = second_full[0]
    value_weight_t = second_full[1]
    current = layer_norm(embedded)
    edge_first = layer_norm(edge_rows) * continues[:, None]
    current_pages = current.reshape(held, PAGE, full_width)
    previous = jnp.concatenate([edge_first[:, None, :], current_pages[:, :-1, :]], axis=1).reshape(
        slot_rows, full_width
    )
    mixed_decay, mixed_key, mixed_value, mixed_query, mixed_gate = mixed_inputs(
        current, previous, lag_blend_coefs, blend_narrowing_map, blend_widening_maps
    )
    fading_multipliers = log_decay(
        mixed_decay, fading_narrowing_map, fading_widening_map, initial_fading_power
    )
    acceptance_lines = jnp.dot(mixed_query, projections[0], preferred_element_type=jnp.float32)
    present_lookups = jnp.dot(mixed_key, projections[1], preferred_element_type=jnp.float32)
    present_contents = jnp.dot(mixed_value, projections[2], preferred_element_type=jnp.float32)
    gate_raw = jnp.dot(mixed_gate, projections[3], preferred_element_type=jnp.float32)
    gating = jax.nn.silu(gate_raw)
    blocks = slot_rows // BLOCK
    per_page = PAGE // BLOCK

    def to_blocks(value_rows):
        return value_rows.reshape(blocks, BLOCK, attenders_on_shard, ATTENTION_DEPTH).transpose(
            0, 2, 1, 3
        )

    block_index = jnp.arange(blocks, dtype=jnp.int32)
    block_start = block_index % per_page == 0
    block_slot = block_index // per_page
    slot_keep = continues * (held_number > 0)
    keep_state = jnp.where(block_start, jnp.take(slot_keep, block_slot), 1.0)
    keep_factor = jnp.where(block_start, jnp.take(continues, block_slot), 1.0)
    attender_extra = present_symbol_extra.reshape(attenders_on_shard, ATTENTION_DEPTH)
    strictly_lower = jnp.arange(BLOCK)[:, None] > jnp.arange(BLOCK)[None, :]

    askers_b = to_blocks(acceptance_lines)
    lookups_b = to_blocks(present_lookups)
    values_b = to_blocks(present_contents)
    decay_b = to_blocks(fading_multipliers)
    inclusive = jnp.cumsum(decay_b, axis=2)
    exclusive = inclusive - decay_b
    query_scaled = askers_b * jnp.exp(exclusive)
    key_scaled = lookups_b * jnp.exp(-inclusive)
    scores = jnp.einsum("bhts,bhus->bhtu", query_scaled, key_scaled, precision=EXACT_ARITHMETIC)
    scores = jnp.where(strictly_lower, scores, 0.0)
    selfpair_contribution = jnp.sum(askers_b * attender_extra[None, :, None, :] * lookups_b, axis=3)
    intra = (
        jnp.einsum("bhtu,bhuj->bhtj", scores, values_b, precision=EXACT_ARITHMETIC)
        + selfpair_contribution[..., None] * values_b
    )
    block_total = inclusive[:, :, -1, :]
    block_decay = jnp.exp(block_total)
    key_end = lookups_b * jnp.exp(block_total[:, :, None, :] - inclusive)
    block_kv = jnp.einsum("bhts,bhtj->bhsj", key_end, values_b, precision=EXACT_ARITHMETIC)
    sweep = jnp.zeros((attenders_on_shard, ATTENTION_DEPTH, ATTENTION_DEPTH), jnp.float32)
    factor = jnp.ones((attenders_on_shard, ATTENTION_DEPTH), jnp.float32)
    starts, factors_before, ends, factors_after = [], [], [], []
    for number in range(blocks):
        sweep = sweep * keep_state[number]
        factor = factor * keep_factor[number]
        starts.append(sweep)
        factors_before.append(factor)
        sweep = block_decay[number][:, :, None] * sweep + block_kv[number]
        factor = factor * block_decay[number]
        ends.append(sweep)
        factors_after.append(factor)
    block_out = intra + jnp.einsum(
        "bhts,bhsj->bhtj", query_scaled, jnp.stack(starts), precision=EXACT_ARITHMETIC
    )
    carry_rows = query_scaled * jnp.stack(factors_before)[:, :, None, :]
    block_states = jnp.stack(ends)
    block_factors = jnp.stack(factors_after)
    page_end = block_states[per_page - 1 :: per_page]
    page_factor = block_factors[per_page - 1 :: per_page]
    leaving_state = page_end[-1]
    leaving_factor = page_factor[-1]

    leaving_pack = jnp.concatenate([leaving_state, leaving_factor[:, None, :]], axis=1)
    arrivals = [passed_along(leaving_pack, "group", distance) for distance in range(1, group_count)]
    incoming = jnp.zeros_like(leaving_state)
    for arrival in reversed(arrivals):
        incoming = arrival[:, ATTENTION_DEPTH, :][:, :, None] * incoming + arrival[:, :ATTENTION_DEPTH, :]
    block_out = block_out + jnp.einsum(
        "bhts,hsj->bhtj", carry_rows, incoming, precision=EXACT_ARITHMETIC
    )
    page_end = page_end + page_factor[:, :, :, None] * incoming[None]
    attended = block_out.transpose(0, 2, 1, 3).reshape(slot_rows, features_on_shard)
    normed = (group_norm(attended) * attender_scaling_coefs * gating).astype(jnp.bfloat16)
    mixer_partial = lax.dot_general(
        normed, output_weight_t, (((1,), (1,)), ((), ())), preferred_element_type=jnp.float32
    ).astype(jnp.bfloat16)
    mixer_owned = hier_reduce_scatter(mixer_partial, "head").astype(jnp.bfloat16)
    mixer_total = hier_all_gather(mixer_owned, "head").astype(jnp.float32)
    residual = (embedded.astype(jnp.float32) + mixer_total).astype(jnp.bfloat16)
    last_residual = residual[slot_rows - 1 : slot_rows]
    arriving = passed_along(last_residual, "group", 1)
    channel_in = layer_norm(residual)
    channel_pages = channel_in.reshape(held, PAGE, full_width)
    edge_two = (
        jnp.concatenate([layer_norm(arriving), channel_pages[:-1, -1, :]], axis=0)
        * continues[:, None]
    )
    channel_prev = jnp.concatenate(
        [edge_two[:, None, :], channel_pages[:, :-1, :]], axis=1
    ).reshape(slot_rows, full_width)
    channel_delta = channel_prev - channel_in
    key_input = (channel_in + channel_delta * lag_blend_coefs[6]).astype(jnp.bfloat16)
    gate_input = (channel_in + channel_delta * lag_blend_coefs[7]).astype(jnp.bfloat16)
    gate_raw_two = jnp.dot(gate_input, projections[4], preferred_element_type=jnp.float32)
    key_raw = jnp.dot(key_input, key_weight, preferred_element_type=jnp.float32)
    squared = jnp.square(jax.nn.relu(key_raw)).astype(jnp.bfloat16)
    channel = hier_reduce_scatter(
        lax.dot_general(
            squared, value_weight_t, (((1,), (1,)), ((), ())), preferred_element_type=jnp.float32
        ).astype(jnp.bfloat16),
        "head",
    )
    gate_two = jax.nn.sigmoid(gate_raw_two)
    residual_local = lax.dynamic_slice_in_dim(
        residual, head_here * features_on_shard, features_on_shard, 1
    )
    hidden = (residual_local.astype(jnp.float32) + gate_two * channel).astype(jnp.bfloat16)
    state_held = page_end.reshape(held, attenders_on_shard, ATTENTION_DEPTH * ATTENTION_DEPTH)
    first_edge = lax.dynamic_slice_in_dim(
        current_pages[:, -1, :], head_here * features_on_shard, features_on_shard, 1
    )
    second_edge = lax.dynamic_slice_in_dim(
        channel_pages[:, -1, :], head_here * features_on_shard, features_on_shard, 1
    )
    edge_held = jnp.stack([first_edge, second_edge], axis=1)
    reach = 2
    shifts = range(-reach, reach + 1)

    def from_neighbours(value):
        return jnp.concatenate(
            [value if shift == 0 else passed_along(value, "group", -shift) for shift in shifts], axis=0
        )

    hidden_near = from_neighbours(hidden.reshape(held, PAGE, features_on_shard))
    state_width = state_held.shape[2]
    record_near = from_neighbours(jnp.concatenate([state_held, edge_held], axis=2))
    state_near = record_near[:, :, :state_width]
    edge_near = record_near[:, :, state_width:]
    slot_page = first_page + slot_number
    source_group = slot_page // held
    source_index = (source_group - group_here + reach) * held + slot_page - source_group * held
    source_index = jnp.clip(source_index, 0, (2 * reach + 1) * held - 1)
    hidden_out = jnp.take(hidden_near, source_index, axis=0)
    hidden_out = jnp.where(slot_live[:, None, None], hidden_out, jnp.zeros_like(hidden_out))
    hidden_out = hidden_out.reshape(SLOTS * PAGE, features_on_shard)
    state_out = jnp.take(state_near, source_index, axis=0)
    state_out = jnp.where(slot_live[:, None, None], state_out, jnp.zeros_like(state_out))
    edge_out = jnp.take(edge_near, source_index, axis=0)
    edge_out = jnp.where(slot_live[:, None, None], edge_out, jnp.zeros_like(edge_out))
    return (hidden_out, state_out, edge_out)


def solution(mesh):
    in_specs = (
        P(None, "head"),
        P(None, "group", "head"),
        P("group", "head"),
        P("head", "group"),
        P("head", "group"),
        P(),
        P(),
        P(),
        P(),
        P(None, "head"),
        P("head"),
        P("head"),
        P("head"),
        P(),
        P(),
        P(),
    )
    out_specs = (P("group", "head"), P("group", "head", None), P("group", None, "head"))
    return jax.shard_map(
        per_device, mesh=mesh, in_specs=in_specs, out_specs=out_specs, check_vma=False
    )
```

```python
import jax
import jax.numpy as jnp
from jax import lax
from jax.sharding import PartitionSpec as P

ATTENTION_DEPTH = 64
PAGE = 256
SLOTS = 4
BLOCK = 128


EXACT_ARITHMETIC = lax.Precision.HIGHEST
LAYER_EPS = 1e-05
GROUP_EPS = 0.00064


def passed_along(value, axis, steps):
    count = lax.axis_size(axis)
    initial, last = (max(0, -steps), min(count, count - steps))
    return lax.ppermute(value, axis, [(source, source + steps) for source in range(initial, last)])


def _swap(value, axis, flip):
    count = lax.axis_size(axis)
    return lax.ppermute(value, axis, [(s, s ^ flip) for s in range(count)])


def _ring(value, axis, step):
    count = lax.axis_size(axis)
    pairs = []
    for s in range(count):
        z = (s // 2) % 4
        target = s - z * 2 + ((z + step) % 4) * 2
        pairs.append((s, target))
    return lax.ppermute(value, axis, pairs)


def hier_reduce_scatter(partial, axis):
    h = lax.axis_index(axis)
    core = h % 2
    z = (h // 2) % 4
    yh = h // 8
    _, rows, width = partial.shape
    blocks = partial.reshape(2, 4, 2, rows, width)
    mine = jnp.where(core == 0, blocks[:, :, 0], blocks[:, :, 1])
    other = jnp.where(core == 0, blocks[:, :, 1], blocks[:, :, 0])
    acc = (mine.astype(jnp.float32) + _swap(other, axis, 1).astype(jnp.float32)).astype(jnp.bfloat16)
    total = jnp.take(acc, z, axis=1).astype(jnp.float32)
    for step in (1, 2, 3):
        send = jnp.take(acc, (z + step) % 4, axis=1)
        total = total + _ring(send, axis, step).astype(jnp.float32)
    total = total.astype(jnp.bfloat16)
    keep = jnp.where(yh == 0, total[0], total[1])
    give = jnp.where(yh == 0, total[1], total[0])
    return keep.astype(jnp.float32) + _swap(give, axis, 8).astype(jnp.float32)


def hier_all_gather(piece, axis):
    h = lax.axis_index(axis)
    core = h % 2
    z = (h // 2) % 4
    yh = h // 8
    got = _swap(piece, axis, 8)
    pair = jnp.where(yh == 0, jnp.stack([piece, got]), jnp.stack([got, piece]))
    ring_parts = [pair] + [_ring(pair, axis, -step % 4) for step in (1, 2, 3)]
    stacked = jnp.stack(ring_parts, 1)
    by_z = jnp.take(stacked, (jnp.arange(4) - z) % 4, axis=1)
    partner = _swap(by_z, axis, 1)
    both = jnp.where(core == 0, jnp.stack([by_z, partner], 2), jnp.stack([partner, by_z], 2))
    return both.reshape((16,) + piece.shape)


def layer_norm(value_rows):
    value_rows = value_rows.astype(jnp.float32)
    centered = value_rows - jnp.mean(value_rows, axis=-1, keepdims=True)
    return centered * lax.rsqrt(jnp.mean(centered * centered, axis=-1, keepdims=True) + LAYER_EPS)


def mixed_inputs(current, previous, lag_blend_coefs, blend_narrowing_map, blend_widening_maps):
    delta_rows = previous - current
    seeded = (current + delta_rows * lag_blend_coefs[0]).astype(jnp.bfloat16)
    low_rank = jnp.tanh(
        jnp.dot(seeded, blend_narrowing_map, preferred_element_type=jnp.float32)
    ).astype(jnp.bfloat16)
    rank_width = blend_widening_maps.shape[1]
    result_lines = []
    for number in range(5):
        column_part = low_rank[:, number * rank_width : (number + 1) * rank_width]
        offset = jnp.dot(
            column_part, blend_widening_maps[number], preferred_element_type=jnp.float32
        )
        result_lines.append(
            (current + delta_rows * (lag_blend_coefs[number + 1] + offset)).astype(jnp.bfloat16)
        )
    return result_lines


def log_decay(mixed_decay, fading_narrowing_map, fading_widening_map, initial_fading_power):
    hidden_low = jnp.tanh(
        jnp.dot(mixed_decay, fading_narrowing_map, preferred_element_type=jnp.float32)
    ).astype(jnp.bfloat16)
    return -jnp.exp(
        initial_fading_power
        + jnp.dot(hidden_low, fading_widening_map, preferred_element_type=jnp.float32)
    )


def group_norm(value_rows):
    shaped = value_rows.reshape(value_rows.shape[0], -1, ATTENTION_DEPTH)
    centered = shaped - jnp.mean(shaped, axis=-1, keepdims=True)
    normed = centered * lax.rsqrt(jnp.mean(centered * centered, axis=-1, keepdims=True) + GROUP_EPS)
    return normed.reshape(value_rows.shape)


def per_device(
    symbol_lookup_table,
    joined_linear_maps,
    feedforward_lookup_map,
    timeblend_result_map,
    feedforward_content_map,
    lag_blend_coefs,
    blend_narrowing_map,
    blend_widening_maps,
    fading_narrowing_map,
    fading_widening_map,
    initial_fading_power,
    present_symbol_extra,
    attender_scaling_coefs,
    active_cluster_sheets,
    sheets_for_inquiry,
    sheet_symbol_indices,
):
    group_count = lax.axis_size("group")
    group_here = lax.axis_index("group")
    head_here = lax.axis_index("head")
    features_on_shard = present_symbol_extra.shape[0]
    attenders_on_shard = features_on_shard // ATTENTION_DEPTH
    held = sheet_symbol_indices.shape[0] // group_count
    slot_rows = held * PAGE
    full_width = lag_blend_coefs.shape[1]
    group_number = jnp.arange(group_count, dtype=jnp.int32)
    pick_group = group_number == group_here
    live_count = jnp.sum(jnp.where(pick_group, active_cluster_sheets, 0))
    group_first = jnp.cumsum(active_cluster_sheets) - active_cluster_sheets
    first_page = jnp.sum(jnp.where(pick_group, group_first, 0))
    slot_number = jnp.arange(SLOTS, dtype=jnp.int32)
    slot_live = slot_number < live_count
    held_number = jnp.arange(held, dtype=jnp.int32)
    request_first = jnp.cumsum(sheets_for_inquiry) - sheets_for_inquiry
    page_here = group_here * held + held_number
    begins = jnp.any(page_here[:, None] == request_first[None, :], axis=1)
    continues = jnp.where(jnp.logical_not(begins), 1.0, 0.0).astype(jnp.float32)
    tokens_here = jnp.take(sheet_symbol_indices, page_here, axis=0)
    before_token = jnp.take(sheet_symbol_indices[:, -1], jnp.maximum(page_here - 1, 0))
    edge_pad = jnp.concatenate([before_token, jnp.zeros((8 - held,), before_token.dtype)])
    all_tokens = jnp.concatenate([tokens_here.reshape(-1), edge_pad])
    own_rows = jnp.take(symbol_lookup_table, all_tokens, axis=0)
    gathered_rows = lax.all_gather(own_rows, "head", axis=1, tiled=True)
    embedded = gathered_rows[:slot_rows]
    edge_rows = gathered_rows[slot_rows : slot_rows + held]
    map_count = joined_linear_maps.shape[0]
    first_pack = jnp.concatenate(
        [joined_linear_maps, timeblend_result_map.T[None]], axis=0
    ).astype(jnp.bfloat16)
    second_pack = jnp.stack(
        [feedforward_lookup_map, feedforward_content_map.T], axis=0
    ).astype(jnp.bfloat16)
    first_pack, _ = lax.optimization_barrier((first_pack, gathered_rows))
    first_full = lax.all_gather(first_pack, "group", axis=1, tiled=True)
    second_pack, _ = lax.optimization_barrier((second_pack, first_full))
    second_full = lax.all_gather(second_pack, "group", axis=1, tiled=True)
    projections = first_full[:map_count]
    output_weight_t = first_full[map_count]
    key_weight = second_full[0]
    value_weight_t = second_full[1]
    current = layer_norm(embedded)
    edge_first = layer_norm(edge_rows) * continues[:, None]
    current_pages = current.reshape(held, PAGE, full_width)
    previous = jnp.concatenate([edge_first[:, None, :], current_pages[:, :-1, :]], axis=1).reshape(
        slot_rows, full_width
    )
    mixed_decay, mixed_key, mixed_value, mixed_query, mixed_gate = mixed_inputs(
        current, previous, lag_blend_coefs, blend_narrowing_map, blend_widening_maps
    )
    fading_multipliers = log_decay(
        mixed_decay, fading_narrowing_map, fading_widening_map, initial_fading_power
    )
    acceptance_lines = jnp.dot(mixed_query, projections[0], preferred_element_type=jnp.float32)
    present_lookups = jnp.dot(mixed_key, projections[1], preferred_element_type=jnp.float32)
    present_contents = jnp.dot(mixed_value, projections[2], preferred_element_type=jnp.float32)
    gate_raw = jnp.dot(mixed_gate, projections[3], preferred_element_type=jnp.float32)
    gating = jax.nn.silu(gate_raw)
    blocks = slot_rows // BLOCK
    per_page = PAGE // BLOCK

    def to_blocks(value_rows):
        return value_rows.reshape(blocks, BLOCK, attenders_on_shard, ATTENTION_DEPTH).transpose(
            0, 2, 1, 3
        )

    block_index = jnp.arange(blocks, dtype=jnp.int32)
    block_start = block_index % per_page == 0
    block_slot = block_index // per_page
    slot_keep = continues * (held_number > 0)
    keep_state = jnp.where(block_start, jnp.take(slot_keep, block_slot), 1.0)
    keep_factor = jnp.where(block_start, jnp.take(continues, block_slot), 1.0)
    attender_extra = present_symbol_extra.reshape(attenders_on_shard, ATTENTION_DEPTH)
    strictly_lower = jnp.arange(BLOCK)[:, None] > jnp.arange(BLOCK)[None, :]

    askers_b = to_blocks(acceptance_lines)
    lookups_b = to_blocks(present_lookups)
    values_b = to_blocks(present_contents)
    decay_b = to_blocks(fading_multipliers)
    inclusive = jnp.cumsum(decay_b, axis=2)
    exclusive = inclusive - decay_b
    query_scaled = askers_b * jnp.exp(exclusive)
    key_scaled = lookups_b * jnp.exp(-inclusive)
    scores = jnp.einsum("bhts,bhus->bhtu", query_scaled, key_scaled, precision=EXACT_ARITHMETIC)
    scores = jnp.where(strictly_lower, scores, 0.0)
    selfpair_contribution = jnp.sum(askers_b * attender_extra[None, :, None, :] * lookups_b, axis=3)
    intra = (
        jnp.einsum("bhtu,bhuj->bhtj", scores, values_b, precision=EXACT_ARITHMETIC)
        + selfpair_contribution[..., None] * values_b
    )
    block_total = inclusive[:, :, -1, :]
    block_decay = jnp.exp(block_total)
    key_end = lookups_b * jnp.exp(block_total[:, :, None, :] - inclusive)
    block_kv = jnp.einsum("bhts,bhtj->bhsj", key_end, values_b, precision=EXACT_ARITHMETIC)
    sweep = jnp.zeros((attenders_on_shard, ATTENTION_DEPTH, ATTENTION_DEPTH), jnp.float32)
    factor = jnp.ones((attenders_on_shard, ATTENTION_DEPTH), jnp.float32)
    starts, factors_before, ends, factors_after = [], [], [], []
    for number in range(blocks):
        sweep = sweep * keep_state[number]
        factor = factor * keep_factor[number]
        starts.append(sweep)
        factors_before.append(factor)
        sweep = block_decay[number][:, :, None] * sweep + block_kv[number]
        factor = factor * block_decay[number]
        ends.append(sweep)
        factors_after.append(factor)
    block_out = intra + jnp.einsum(
        "bhts,bhsj->bhtj", query_scaled, jnp.stack(starts), precision=EXACT_ARITHMETIC
    )
    carry_rows = query_scaled * jnp.stack(factors_before)[:, :, None, :]
    block_states = jnp.stack(ends)
    block_factors = jnp.stack(factors_after)
    page_end = block_states[per_page - 1 :: per_page]
    page_factor = block_factors[per_page - 1 :: per_page]
    leaving_state = page_end[-1]
    leaving_factor = page_factor[-1]

    leaving_pack = jnp.concatenate([leaving_state, leaving_factor[:, None, :]], axis=1)
    arrivals = [passed_along(leaving_pack, "group", distance) for distance in range(1, group_count)]
    incoming = jnp.zeros_like(leaving_state)
    for arrival in reversed(arrivals):
        incoming = arrival[:, ATTENTION_DEPTH, :][:, :, None] * incoming + arrival[:, :ATTENTION_DEPTH, :]
    block_out = block_out + jnp.einsum(
        "bhts,hsj->bhtj", carry_rows, incoming, precision=EXACT_ARITHMETIC
    )
    page_end = page_end + page_factor[:, :, :, None] * incoming[None]
    attended = block_out.transpose(0, 2, 1, 3).reshape(slot_rows, features_on_shard)
    normed = (group_norm(attended) * attender_scaling_coefs * gating).astype(jnp.bfloat16)
    head_count = lax.axis_size("head")
    mixer_partial = jnp.einsum(
        "rc,bfc->brf",
        normed,
        output_weight_t.reshape(head_count, -1, output_weight_t.shape[1]),
        preferred_element_type=jnp.float32,
    ).astype(jnp.bfloat16)
    mixer_owned = hier_reduce_scatter(mixer_partial, "head").astype(jnp.bfloat16)
    mixer_total = (
        hier_all_gather(mixer_owned, "head").transpose(1, 0, 2).reshape(slot_rows, full_width)
    ).astype(jnp.float32)
    residual = (embedded.astype(jnp.float32) + mixer_total).astype(jnp.bfloat16)
    last_residual = residual[slot_rows - 1 : slot_rows]
    arriving = passed_along(last_residual, "group", 1)
    channel_in = layer_norm(residual)
    channel_pages = channel_in.reshape(held, PAGE, full_width)
    edge_two = (
        jnp.concatenate([layer_norm(arriving), channel_pages[:-1, -1, :]], axis=0)
        * continues[:, None]
    )
    channel_prev = jnp.concatenate(
        [edge_two[:, None, :], channel_pages[:, :-1, :]], axis=1
    ).reshape(slot_rows, full_width)
    channel_delta = channel_prev - channel_in
    key_input = (channel_in + channel_delta * lag_blend_coefs[6]).astype(jnp.bfloat16)
    gate_input = (channel_in + channel_delta * lag_blend_coefs[7]).astype(jnp.bfloat16)
    gate_raw_two = jnp.dot(gate_input, projections[4], preferred_element_type=jnp.float32)
    key_raw = jnp.dot(key_input, key_weight, preferred_element_type=jnp.float32)
    squared = jnp.square(jax.nn.relu(key_raw)).astype(jnp.bfloat16)
    channel = hier_reduce_scatter(
        jnp.einsum(
            "rk,bfk->brf",
            squared,
            value_weight_t.reshape(head_count, -1, value_weight_t.shape[1]),
            preferred_element_type=jnp.float32,
        ).astype(jnp.bfloat16),
        "head",
    )
    gate_two = jax.nn.sigmoid(gate_raw_two)
    residual_local = lax.dynamic_slice_in_dim(
        residual, head_here * features_on_shard, features_on_shard, 1
    )
    hidden = (residual_local.astype(jnp.float32) + gate_two * channel).astype(jnp.bfloat16)
    state_held = page_end.reshape(held, attenders_on_shard, ATTENTION_DEPTH * ATTENTION_DEPTH)
    first_edge = lax.dynamic_slice_in_dim(
        current_pages[:, -1, :], head_here * features_on_shard, features_on_shard, 1
    )
    second_edge = lax.dynamic_slice_in_dim(
        channel_pages[:, -1, :], head_here * features_on_shard, features_on_shard, 1
    )
    edge_held = jnp.stack([first_edge, second_edge], axis=1)
    reach = 2
    shifts = range(-reach, reach + 1)

    def from_neighbours(value):
        return jnp.concatenate(
            [value if shift == 0 else passed_along(value, "group", -shift) for shift in shifts], axis=0
        )

    hidden_near = from_neighbours(hidden.reshape(held, PAGE, features_on_shard))
    state_near = from_neighbours(state_held)
    edge_near = from_neighbours(edge_held)
    slot_page = first_page + slot_number
    source_group = slot_page // held
    source_index = (source_group - group_here + reach) * held + slot_page - source_group * held
    source_index = jnp.clip(source_index, 0, (2 * reach + 1) * held - 1)
    hidden_out = jnp.take(hidden_near, source_index, axis=0)
    hidden_out = jnp.where(slot_live[:, None, None], hidden_out, jnp.zeros_like(hidden_out))
    hidden_out = hidden_out.reshape(SLOTS * PAGE, features_on_shard)
    state_out = jnp.take(state_near, source_index, axis=0)
    state_out = jnp.where(slot_live[:, None, None], state_out, jnp.zeros_like(state_out))
    edge_out = jnp.take(edge_near, source_index, axis=0)
    edge_out = jnp.where(slot_live[:, None, None], edge_out, jnp.zeros_like(edge_out))
    return (hidden_out, state_out, edge_out)


def solution(mesh):
    in_specs = (
        P(None, "head"),
        P(None, "group", "head"),
        P("group", "head"),
        P("head", "group"),
        P("head", "group"),
        P(),
        P(),
        P(),
        P(),
        P(None, "head"),
        P("head"),
        P("head"),
        P("head"),
        P(),
        P(),
        P(),
    )
    out_specs = (P("group", "head"), P("group", "head", None), P("group", None, "head"))
    return jax.shard_map(
        per_device, mesh=mesh, in_specs=in_specs, out_specs=out_specs, check_vma=False
    )
```

```python
import jax
import jax.numpy as jnp
from jax import lax
from jax.sharding import PartitionSpec as P

ATTENTION_DEPTH = 64
PAGE = 256
SLOTS = 4
BLOCK = 128


EXACT_ARITHMETIC = lax.Precision.HIGHEST
LAYER_EPS = 1e-05
GROUP_EPS = 0.00064


def passed_along(value, axis, steps):
    count = lax.axis_size(axis)
    initial, last = (max(0, -steps), min(count, count - steps))
    return lax.ppermute(value, axis, [(source, source + steps) for source in range(initial, last)])


def _swap(value, axis, flip):
    count = lax.axis_size(axis)
    return lax.ppermute(value, axis, [(s, s ^ flip) for s in range(count)])


def _ring(value, axis, step):
    count = lax.axis_size(axis)
    pairs = []
    for s in range(count):
        z = (s // 2) % 4
        target = s - z * 2 + ((z + step) % 4) * 2
        pairs.append((s, target))
    return lax.ppermute(value, axis, pairs)


def hier_reduce_scatter(partial, axis):
    h = lax.axis_index(axis)
    core = h % 2
    z = (h // 2) % 4
    yh = h // 8
    _, rows, width = partial.shape
    blocks = partial.reshape(2, 4, 2, rows, width)
    mine = jnp.where(core == 0, blocks[:, :, 0], blocks[:, :, 1])
    other = jnp.where(core == 0, blocks[:, :, 1], blocks[:, :, 0])
    acc = (mine.astype(jnp.float32) + _swap(other, axis, 1).astype(jnp.float32)).astype(jnp.bfloat16)
    total = jnp.take(acc, z, axis=1).astype(jnp.float32)
    for step in (1, 2, 3):
        send = jnp.take(acc, (z + step) % 4, axis=1)
        total = total + _ring(send, axis, step).astype(jnp.float32)
    total = total.astype(jnp.bfloat16)
    keep = jnp.where(yh == 0, total[0], total[1])
    give = jnp.where(yh == 0, total[1], total[0])
    return keep.astype(jnp.float32) + _swap(give, axis, 8).astype(jnp.float32)


def hier_all_gather(piece, axis):
    h = lax.axis_index(axis)
    core = h % 2
    z = (h // 2) % 4
    yh = h // 8
    got = _swap(piece, axis, 8)
    pair = jnp.where(yh == 0, jnp.stack([piece, got]), jnp.stack([got, piece]))
    ring_parts = [pair] + [_ring(pair, axis, -step % 4) for step in (1, 2, 3)]
    stacked = jnp.stack(ring_parts, 1)
    by_z = jnp.take(stacked, (jnp.arange(4) - z) % 4, axis=1)
    partner = _swap(by_z, axis, 1)
    both = jnp.where(core == 0, jnp.stack([by_z, partner], 2), jnp.stack([partner, by_z], 2))
    return both.reshape((16,) + piece.shape)


def layer_norm(value_rows):
    value_rows = value_rows.astype(jnp.float32)
    centered = value_rows - jnp.mean(value_rows, axis=-1, keepdims=True)
    return centered * lax.rsqrt(jnp.mean(centered * centered, axis=-1, keepdims=True) + LAYER_EPS)


def mixed_inputs(current, previous, lag_blend_coefs, blend_narrowing_map, blend_widening_maps):
    delta_rows = previous - current
    seeded = (current + delta_rows * lag_blend_coefs[0]).astype(jnp.bfloat16)
    low_rank = jnp.tanh(
        jnp.dot(seeded, blend_narrowing_map, preferred_element_type=jnp.float32)
    ).astype(jnp.bfloat16)
    rank_width = blend_widening_maps.shape[1]
    result_lines = []
    for number in range(5):
        column_part = low_rank[:, number * rank_width : (number + 1) * rank_width]
        offset = jnp.dot(
            column_part, blend_widening_maps[number], preferred_element_type=jnp.float32
        )
        result_lines.append(
            (current + delta_rows * (lag_blend_coefs[number + 1] + offset)).astype(jnp.bfloat16)
        )
    return result_lines


def log_decay(mixed_decay, fading_narrowing_map, fading_widening_map, initial_fading_power):
    hidden_low = jnp.tanh(
        jnp.dot(mixed_decay, fading_narrowing_map, preferred_element_type=jnp.float32)
    ).astype(jnp.bfloat16)
    return -jnp.exp(
        initial_fading_power
        + jnp.dot(hidden_low, fading_widening_map, preferred_element_type=jnp.float32)
    )


def group_norm(value_rows):
    shaped = value_rows.reshape(value_rows.shape[0], -1, ATTENTION_DEPTH)
    centered = shaped - jnp.mean(shaped, axis=-1, keepdims=True)
    normed = centered * lax.rsqrt(jnp.mean(centered * centered, axis=-1, keepdims=True) + GROUP_EPS)
    return normed.reshape(value_rows.shape)


def per_device(
    symbol_lookup_table,
    joined_linear_maps,
    feedforward_lookup_map,
    timeblend_result_map,
    feedforward_content_map,
    lag_blend_coefs,
    blend_narrowing_map,
    blend_widening_maps,
    fading_narrowing_map,
    fading_widening_map,
    initial_fading_power,
    present_symbol_extra,
    attender_scaling_coefs,
    active_cluster_sheets,
    sheets_for_inquiry,
    sheet_symbol_indices,
):
    group_count = lax.axis_size("group")
    group_here = lax.axis_index("group")
    head_here = lax.axis_index("head")
    features_on_shard = present_symbol_extra.shape[0]
    attenders_on_shard = features_on_shard // ATTENTION_DEPTH
    held = sheet_symbol_indices.shape[0] // group_count
    slot_rows = held * PAGE
    full_width = lag_blend_coefs.shape[1]
    group_number = jnp.arange(group_count, dtype=jnp.int32)
    pick_group = group_number == group_here
    live_count = jnp.sum(jnp.where(pick_group, active_cluster_sheets, 0))
    group_first = jnp.cumsum(active_cluster_sheets) - active_cluster_sheets
    first_page = jnp.sum(jnp.where(pick_group, group_first, 0))
    slot_number = jnp.arange(SLOTS, dtype=jnp.int32)
    slot_live = slot_number < live_count
    held_number = jnp.arange(held, dtype=jnp.int32)
    request_first = jnp.cumsum(sheets_for_inquiry) - sheets_for_inquiry
    page_here = group_here * held + held_number
    begins = jnp.any(page_here[:, None] == request_first[None, :], axis=1)
    continues = jnp.where(jnp.logical_not(begins), 1.0, 0.0).astype(jnp.float32)
    tokens_here = jnp.take(sheet_symbol_indices, page_here, axis=0)
    before_token = jnp.take(sheet_symbol_indices[:, -1], jnp.maximum(page_here - 1, 0))
    edge_pad = jnp.concatenate([before_token, jnp.zeros((8 - held,), before_token.dtype)])
    all_tokens = jnp.concatenate([tokens_here.reshape(-1), edge_pad])
    own_rows = jnp.take(symbol_lookup_table, all_tokens, axis=0)
    gathered_rows = lax.all_gather(own_rows, "head", axis=1, tiled=True)
    embedded = gathered_rows[:slot_rows]
    edge_rows = gathered_rows[slot_rows : slot_rows + held]
    map_count = joined_linear_maps.shape[0]
    first_pack = jnp.concatenate(
        [joined_linear_maps, timeblend_result_map.T[None]], axis=0
    ).astype(jnp.bfloat16)
    second_pack = jnp.stack(
        [feedforward_lookup_map, feedforward_content_map.T], axis=0
    ).astype(jnp.bfloat16)
    first_pack, _ = lax.optimization_barrier((first_pack, gathered_rows))
    first_full = lax.all_gather(first_pack, "group", axis=1, tiled=True)
    second_pack, _ = lax.optimization_barrier((second_pack, first_full))
    second_full = lax.all_gather(second_pack, "group", axis=1, tiled=True)
    projections = first_full[:map_count]
    output_weight_t = first_full[map_count]
    key_weight = second_full[0]
    value_weight_t = second_full[1]
    current = layer_norm(embedded)
    edge_first = layer_norm(edge_rows) * continues[:, None]
    current_pages = current.reshape(held, PAGE, full_width)
    previous = jnp.concatenate([edge_first[:, None, :], current_pages[:, :-1, :]], axis=1).reshape(
        slot_rows, full_width
    )
    mixed_decay, mixed_key, mixed_value, mixed_query, mixed_gate = mixed_inputs(
        current, previous, lag_blend_coefs, blend_narrowing_map, blend_widening_maps
    )
    fading_multipliers = log_decay(
        mixed_decay, fading_narrowing_map, fading_widening_map, initial_fading_power
    )
    acceptance_lines = jnp.dot(mixed_query, projections[0], preferred_element_type=jnp.float32)
    present_lookups = jnp.dot(mixed_key, projections[1], preferred_element_type=jnp.float32)
    present_contents = jnp.dot(mixed_value, projections[2], preferred_element_type=jnp.float32)
    gate_raw = jnp.dot(mixed_gate, projections[3], preferred_element_type=jnp.float32)
    gating = jax.nn.silu(gate_raw)
    blocks = slot_rows // BLOCK
    per_page = PAGE // BLOCK

    def to_blocks(value_rows):
        return value_rows.reshape(blocks, BLOCK, attenders_on_shard, ATTENTION_DEPTH).transpose(
            0, 2, 1, 3
        )

    block_index = jnp.arange(blocks, dtype=jnp.int32)
    block_start = block_index % per_page == 0
    block_slot = block_index // per_page
    slot_keep = continues * (held_number > 0)
    keep_state = jnp.where(block_start, jnp.take(slot_keep, block_slot), 1.0)
    keep_factor = jnp.where(block_start, jnp.take(continues, block_slot), 1.0)
    attender_extra = present_symbol_extra.reshape(attenders_on_shard, ATTENTION_DEPTH)
    strictly_lower = jnp.arange(BLOCK)[:, None] > jnp.arange(BLOCK)[None, :]

    askers_b = to_blocks(acceptance_lines)
    lookups_b = to_blocks(present_lookups)
    values_b = to_blocks(present_contents)
    decay_b = to_blocks(fading_multipliers)
    inclusive = jnp.cumsum(decay_b, axis=2)
    exclusive = inclusive - decay_b
    query_scaled = askers_b * jnp.exp(exclusive)
    key_scaled = lookups_b * jnp.exp(-inclusive)
    scores = jnp.einsum("bhts,bhus->bhtu", query_scaled, key_scaled, precision=EXACT_ARITHMETIC)
    scores = jnp.where(strictly_lower, scores, 0.0)
    selfpair_contribution = jnp.sum(askers_b * attender_extra[None, :, None, :] * lookups_b, axis=3)
    intra = (
        jnp.einsum("bhtu,bhuj->bhtj", scores, values_b, precision=EXACT_ARITHMETIC)
        + selfpair_contribution[..., None] * values_b
    )
    block_total = inclusive[:, :, -1, :]
    block_decay = jnp.exp(block_total)
    key_end = lookups_b * jnp.exp(block_total[:, :, None, :] - inclusive)
    block_kv = jnp.einsum("bhts,bhtj->bhsj", key_end, values_b, precision=EXACT_ARITHMETIC)
    sweep = jnp.zeros((attenders_on_shard, ATTENTION_DEPTH, ATTENTION_DEPTH), jnp.float32)
    factor = jnp.ones((attenders_on_shard, ATTENTION_DEPTH), jnp.float32)
    starts, factors_before, ends, factors_after = [], [], [], []
    for number in range(blocks):
        sweep = sweep * keep_state[number]
        factor = factor * keep_factor[number]
        starts.append(sweep)
        factors_before.append(factor)
        sweep = block_decay[number][:, :, None] * sweep + block_kv[number]
        factor = factor * block_decay[number]
        ends.append(sweep)
        factors_after.append(factor)
    block_out = intra + jnp.einsum(
        "bhts,bhsj->bhtj", query_scaled, jnp.stack(starts), precision=EXACT_ARITHMETIC
    )
    carry_rows = query_scaled * jnp.stack(factors_before)[:, :, None, :]
    block_states = jnp.stack(ends)
    block_factors = jnp.stack(factors_after)
    page_end = block_states[per_page - 1 :: per_page]
    page_factor = block_factors[per_page - 1 :: per_page]
    leaving_state = page_end[-1]
    leaving_factor = page_factor[-1]

    leaving_pack = jnp.concatenate([leaving_state, leaving_factor[:, None, :]], axis=1)
    arrivals = [passed_along(leaving_pack, "group", distance) for distance in range(1, group_count)]
    incoming = jnp.zeros_like(leaving_state)
    for arrival in reversed(arrivals):
        incoming = arrival[:, ATTENTION_DEPTH, :][:, :, None] * incoming + arrival[:, :ATTENTION_DEPTH, :]
    block_out = block_out + jnp.einsum(
        "bhts,hsj->bhtj", carry_rows, incoming, precision=EXACT_ARITHMETIC
    )
    page_end = page_end + page_factor[:, :, :, None] * incoming[None]
    attended = block_out.transpose(0, 2, 1, 3).reshape(slot_rows, features_on_shard)
    normed = (group_norm(attended) * attender_scaling_coefs * gating).astype(jnp.bfloat16)
    head_count = lax.axis_size("head")
    mixer_partial = jnp.einsum(
        "rc,bfc->brf",
        normed,
        output_weight_t.reshape(head_count, -1, output_weight_t.shape[1]),
        preferred_element_type=jnp.float32,
    ).astype(jnp.bfloat16)
    mixer_partial, _ = lax.optimization_barrier((mixer_partial, second_full))
    mixer_owned = hier_reduce_scatter(mixer_partial, "head").astype(jnp.bfloat16)
    mixer_total = (
        hier_all_gather(mixer_owned, "head").transpose(1, 0, 2).reshape(slot_rows, full_width)
    ).astype(jnp.float32)
    residual = (embedded.astype(jnp.float32) + mixer_total).astype(jnp.bfloat16)
    last_residual = residual[slot_rows - 1 : slot_rows]
    arriving = passed_along(last_residual, "group", 1)
    channel_in = layer_norm(residual)
    channel_pages = channel_in.reshape(held, PAGE, full_width)
    edge_two = (
        jnp.concatenate([layer_norm(arriving), channel_pages[:-1, -1, :]], axis=0)
        * continues[:, None]
    )
    channel_prev = jnp.concatenate(
        [edge_two[:, None, :], channel_pages[:, :-1, :]], axis=1
    ).reshape(slot_rows, full_width)
    channel_delta = channel_prev - channel_in
    key_input = (channel_in + channel_delta * lag_blend_coefs[6]).astype(jnp.bfloat16)
    gate_input = (channel_in + channel_delta * lag_blend_coefs[7]).astype(jnp.bfloat16)
    gate_raw_two = jnp.dot(gate_input, projections[4], preferred_element_type=jnp.float32)
    key_raw = jnp.dot(key_input, key_weight, preferred_element_type=jnp.float32)
    squared = jnp.square(jax.nn.relu(key_raw)).astype(jnp.bfloat16)
    channel = hier_reduce_scatter(
        jnp.einsum(
            "rk,bfk->brf",
            squared,
            value_weight_t.reshape(head_count, -1, value_weight_t.shape[1]),
            preferred_element_type=jnp.float32,
        ).astype(jnp.bfloat16),
        "head",
    )
    gate_two = jax.nn.sigmoid(gate_raw_two)
    residual_local = lax.dynamic_slice_in_dim(
        residual, head_here * features_on_shard, features_on_shard, 1
    )
    hidden = (residual_local.astype(jnp.float32) + gate_two * channel).astype(jnp.bfloat16)
    state_held = page_end.reshape(held, attenders_on_shard, ATTENTION_DEPTH * ATTENTION_DEPTH)
    first_edge = lax.dynamic_slice_in_dim(
        current_pages[:, -1, :], head_here * features_on_shard, features_on_shard, 1
    )
    second_edge = lax.dynamic_slice_in_dim(
        channel_pages[:, -1, :], head_here * features_on_shard, features_on_shard, 1
    )
    edge_held = jnp.stack([first_edge, second_edge], axis=1)
    reach = 2
    shifts = range(-reach, reach + 1)

    def from_neighbours(value):
        return jnp.concatenate(
            [value if shift == 0 else passed_along(value, "group", -shift) for shift in shifts], axis=0
        )

    hidden_near = from_neighbours(hidden.reshape(held, PAGE, features_on_shard))
    state_near = from_neighbours(state_held)
    edge_near = from_neighbours(edge_held)
    slot_page = first_page + slot_number
    source_group = slot_page // held
    source_index = (source_group - group_here + reach) * held + slot_page - source_group * held
    source_index = jnp.clip(source_index, 0, (2 * reach + 1) * held - 1)
    hidden_out = jnp.take(hidden_near, source_index, axis=0)
    hidden_out = jnp.where(slot_live[:, None, None], hidden_out, jnp.zeros_like(hidden_out))
    hidden_out = hidden_out.reshape(SLOTS * PAGE, features_on_shard)
    state_out = jnp.take(state_near, source_index, axis=0)
    state_out = jnp.where(slot_live[:, None, None], state_out, jnp.zeros_like(state_out))
    edge_out = jnp.take(edge_near, source_index, axis=0)
    edge_out = jnp.where(slot_live[:, None, None], edge_out, jnp.zeros_like(edge_out))
    return (hidden_out, state_out, edge_out)


def solution(mesh):
    in_specs = (
        P(None, "head"),
        P(None, "group", "head"),
        P("group", "head"),
        P("head", "group"),
        P("head", "group"),
        P(),
        P(),
        P(),
        P(),
        P(None, "head"),
        P("head"),
        P("head"),
        P("head"),
        P(),
        P(),
        P(),
    )
    out_specs = (P("group", "head"), P("group", "head", None), P("group", None, "head"))
    return jax.shard_map(
        per_device, mesh=mesh, in_specs=in_specs, out_specs=out_specs, check_vma=False
    )
```

```python
import jax
import jax.numpy as jnp
from jax import lax
from jax.sharding import PartitionSpec as P

ATTENTION_DEPTH = 64
PAGE = 256
SLOTS = 4
BLOCK = 128


EXACT_ARITHMETIC = lax.Precision.HIGHEST
LAYER_EPS = 1e-05
GROUP_EPS = 0.00064


def passed_along(value, axis, steps):
    count = lax.axis_size(axis)
    initial, last = (max(0, -steps), min(count, count - steps))
    return lax.ppermute(value, axis, [(source, source + steps) for source in range(initial, last)])


def _swap(value, axis, flip):
    count = lax.axis_size(axis)
    return lax.ppermute(value, axis, [(s, s ^ flip) for s in range(count)])


def _ring(value, axis, step):
    count = lax.axis_size(axis)
    pairs = []
    for s in range(count):
        z = (s // 2) % 4
        target = s - z * 2 + ((z + step) % 4) * 2
        pairs.append((s, target))
    return lax.ppermute(value, axis, pairs)


def hier_reduce_scatter(partial, axis):
    h = lax.axis_index(axis)
    core = h % 2
    z = (h // 2) % 4
    yh = h // 8
    _, rows, width = partial.shape
    blocks = partial.reshape(2, 4, 2, rows, width)
    mine = jnp.where(core == 0, blocks[:, :, 0], blocks[:, :, 1])
    other = jnp.where(core == 0, blocks[:, :, 1], blocks[:, :, 0])
    acc = (mine.astype(jnp.float32) + _swap(other, axis, 1).astype(jnp.float32)).astype(jnp.bfloat16)
    total = jnp.take(acc, z, axis=1).astype(jnp.float32)
    for step in (1, 2, 3):
        send = jnp.take(acc, (z + step) % 4, axis=1)
        total = total + _ring(send, axis, step).astype(jnp.float32)
    total = total.astype(jnp.bfloat16)
    keep = jnp.where(yh == 0, total[0], total[1])
    give = jnp.where(yh == 0, total[1], total[0])
    return keep.astype(jnp.float32) + _swap(give, axis, 8).astype(jnp.float32)


def hier_all_gather(piece, axis):
    h = lax.axis_index(axis)
    core = h % 2
    z = (h // 2) % 4
    yh = h // 8
    got = _swap(piece, axis, 8)
    pair = jnp.where(yh == 0, jnp.stack([piece, got]), jnp.stack([got, piece]))
    ring_parts = [pair] + [_ring(pair, axis, -step % 4) for step in (1, 2, 3)]
    stacked = jnp.stack(ring_parts, 1)
    by_z = jnp.take(stacked, (jnp.arange(4) - z) % 4, axis=1)
    partner = _swap(by_z, axis, 1)
    both = jnp.where(core == 0, jnp.stack([by_z, partner], 2), jnp.stack([partner, by_z], 2))
    return both.reshape((16,) + piece.shape)


def layer_norm(value_rows):
    value_rows = value_rows.astype(jnp.float32)
    centered = value_rows - jnp.mean(value_rows, axis=-1, keepdims=True)
    return centered * lax.rsqrt(jnp.mean(centered * centered, axis=-1, keepdims=True) + LAYER_EPS)


def mixed_inputs(current, previous, lag_blend_coefs, blend_narrowing_map, blend_widening_maps):
    delta_rows = previous - current
    seeded = (current + delta_rows * lag_blend_coefs[0]).astype(jnp.bfloat16)
    low_rank = jnp.tanh(
        jnp.dot(seeded, blend_narrowing_map, preferred_element_type=jnp.float32)
    ).astype(jnp.bfloat16)
    rank_width = blend_widening_maps.shape[1]
    result_lines = []
    for number in range(5):
        column_part = low_rank[:, number * rank_width : (number + 1) * rank_width]
        offset = jnp.dot(
            column_part, blend_widening_maps[number], preferred_element_type=jnp.float32
        )
        result_lines.append(
            (current + delta_rows * (lag_blend_coefs[number + 1] + offset)).astype(jnp.bfloat16)
        )
    return result_lines


def log_decay(mixed_decay, fading_narrowing_map, fading_widening_map, initial_fading_power):
    hidden_low = jnp.tanh(
        jnp.dot(mixed_decay, fading_narrowing_map, preferred_element_type=jnp.float32)
    ).astype(jnp.bfloat16)
    return -jnp.exp(
        initial_fading_power
        + jnp.dot(hidden_low, fading_widening_map, preferred_element_type=jnp.float32)
    )


def group_norm(value_rows):
    shaped = value_rows.reshape(value_rows.shape[0], -1, ATTENTION_DEPTH)
    centered = shaped - jnp.mean(shaped, axis=-1, keepdims=True)
    normed = centered * lax.rsqrt(jnp.mean(centered * centered, axis=-1, keepdims=True) + GROUP_EPS)
    return normed.reshape(value_rows.shape)


def per_device(
    symbol_lookup_table,
    joined_linear_maps,
    feedforward_lookup_map,
    timeblend_result_map,
    feedforward_content_map,
    lag_blend_coefs,
    blend_narrowing_map,
    blend_widening_maps,
    fading_narrowing_map,
    fading_widening_map,
    initial_fading_power,
    present_symbol_extra,
    attender_scaling_coefs,
    active_cluster_sheets,
    sheets_for_inquiry,
    sheet_symbol_indices,
):
    group_count = lax.axis_size("group")
    group_here = lax.axis_index("group")
    head_here = lax.axis_index("head")
    features_on_shard = present_symbol_extra.shape[0]
    attenders_on_shard = features_on_shard // ATTENTION_DEPTH
    held = sheet_symbol_indices.shape[0] // group_count
    slot_rows = held * PAGE
    full_width = lag_blend_coefs.shape[1]
    group_number = jnp.arange(group_count, dtype=jnp.int32)
    pick_group = group_number == group_here
    live_count = jnp.sum(jnp.where(pick_group, active_cluster_sheets, 0))
    group_first = jnp.cumsum(active_cluster_sheets) - active_cluster_sheets
    first_page = jnp.sum(jnp.where(pick_group, group_first, 0))
    slot_number = jnp.arange(SLOTS, dtype=jnp.int32)
    slot_live = slot_number < live_count
    held_number = jnp.arange(held, dtype=jnp.int32)
    request_first = jnp.cumsum(sheets_for_inquiry) - sheets_for_inquiry
    page_here = group_here * held + held_number
    begins = jnp.any(page_here[:, None] == request_first[None, :], axis=1)
    continues = jnp.where(jnp.logical_not(begins), 1.0, 0.0).astype(jnp.float32)
    tokens_here = jnp.take(sheet_symbol_indices, page_here, axis=0)
    before_token = jnp.take(sheet_symbol_indices[:, -1], jnp.maximum(page_here - 1, 0))
    edge_pad = jnp.concatenate([before_token, jnp.zeros((8 - held,), before_token.dtype)])
    all_tokens = jnp.concatenate([tokens_here.reshape(-1), edge_pad])
    own_rows = jnp.take(symbol_lookup_table, all_tokens, axis=0)
    gathered_rows = lax.all_gather(own_rows, "head", axis=1, tiled=True)
    embedded = gathered_rows[:slot_rows]
    edge_rows = gathered_rows[slot_rows : slot_rows + held]
    map_count = joined_linear_maps.shape[0]
    first_pack = jnp.concatenate(
        [joined_linear_maps, timeblend_result_map.T[None]], axis=0
    ).astype(jnp.bfloat16)
    second_pack = jnp.stack(
        [feedforward_lookup_map, feedforward_content_map.T], axis=0
    ).astype(jnp.bfloat16)
    first_pack, _ = lax.optimization_barrier((first_pack, gathered_rows))
    first_full = lax.all_gather(first_pack, "group", axis=1, tiled=True)
    second_pack, _ = lax.optimization_barrier((second_pack, first_full))
    second_full = lax.all_gather(second_pack, "group", axis=1, tiled=True)
    projections = first_full[:map_count]
    output_weight_t = first_full[map_count]
    key_weight = second_full[0]
    value_weight_t = second_full[1]
    current = layer_norm(embedded)
    edge_first = layer_norm(edge_rows) * continues[:, None]
    current_pages = current.reshape(held, PAGE, full_width)
    previous = jnp.concatenate([edge_first[:, None, :], current_pages[:, :-1, :]], axis=1).reshape(
        slot_rows, full_width
    )
    mixed_decay, mixed_key, mixed_value, mixed_query, mixed_gate = mixed_inputs(
        current, previous, lag_blend_coefs, blend_narrowing_map, blend_widening_maps
    )
    fading_multipliers = log_decay(
        mixed_decay, fading_narrowing_map, fading_widening_map, initial_fading_power
    )
    acceptance_lines = jnp.dot(mixed_query, projections[0], preferred_element_type=jnp.float32)
    present_lookups = jnp.dot(mixed_key, projections[1], preferred_element_type=jnp.float32)
    present_contents = jnp.dot(mixed_value, projections[2], preferred_element_type=jnp.float32)
    gate_raw = jnp.dot(mixed_gate, projections[3], preferred_element_type=jnp.float32)
    gating = jax.nn.silu(gate_raw)
    blocks = slot_rows // BLOCK
    per_page = PAGE // BLOCK

    def to_blocks(value_rows):
        return value_rows.reshape(blocks, BLOCK, attenders_on_shard, ATTENTION_DEPTH).transpose(
            0, 2, 1, 3
        )

    block_index = jnp.arange(blocks, dtype=jnp.int32)
    block_start = block_index % per_page == 0
    block_slot = block_index // per_page
    slot_keep = continues * (held_number > 0)
    keep_state = jnp.where(block_start, jnp.take(slot_keep, block_slot), 1.0)
    keep_factor = jnp.where(block_start, jnp.take(continues, block_slot), 1.0)
    attender_extra = present_symbol_extra.reshape(attenders_on_shard, ATTENTION_DEPTH)
    strictly_lower = jnp.arange(BLOCK)[:, None] > jnp.arange(BLOCK)[None, :]

    askers_b = to_blocks(acceptance_lines)
    lookups_b = to_blocks(present_lookups)
    values_b = to_blocks(present_contents)
    decay_b = to_blocks(fading_multipliers)
    inclusive = jnp.cumsum(decay_b, axis=2)
    exclusive = inclusive - decay_b
    query_scaled = askers_b * jnp.exp(exclusive)
    key_scaled = lookups_b * jnp.exp(-inclusive)
    scores = jnp.einsum("bhts,bhus->bhtu", query_scaled, key_scaled, precision=EXACT_ARITHMETIC)
    scores = jnp.where(strictly_lower, scores, 0.0)
    selfpair_contribution = jnp.sum(askers_b * attender_extra[None, :, None, :] * lookups_b, axis=3)
    intra = (
        jnp.einsum("bhtu,bhuj->bhtj", scores, values_b, precision=EXACT_ARITHMETIC)
        + selfpair_contribution[..., None] * values_b
    )
    block_total = inclusive[:, :, -1, :]
    block_decay = jnp.exp(block_total)
    key_end = lookups_b * jnp.exp(block_total[:, :, None, :] - inclusive)
    block_kv = jnp.einsum("bhts,bhtj->bhsj", key_end, values_b, precision=EXACT_ARITHMETIC)
    sweep = jnp.zeros((attenders_on_shard, ATTENTION_DEPTH, ATTENTION_DEPTH), jnp.float32)
    factor = jnp.ones((attenders_on_shard, ATTENTION_DEPTH), jnp.float32)
    starts, factors_before, ends, factors_after = [], [], [], []
    for number in range(blocks):
        sweep = sweep * keep_state[number]
        factor = factor * keep_factor[number]
        starts.append(sweep)
        factors_before.append(factor)
        sweep = block_decay[number][:, :, None] * sweep + block_kv[number]
        factor = factor * block_decay[number]
        ends.append(sweep)
        factors_after.append(factor)
    block_out = intra + jnp.einsum(
        "bhts,bhsj->bhtj", query_scaled, jnp.stack(starts), precision=EXACT_ARITHMETIC
    )
    carry_rows = query_scaled * jnp.stack(factors_before)[:, :, None, :]
    block_states = jnp.stack(ends)
    block_factors = jnp.stack(factors_after)
    page_end = block_states[per_page - 1 :: per_page]
    page_factor = block_factors[per_page - 1 :: per_page]
    leaving_state = page_end[-1]
    leaving_factor = page_factor[-1]

    leaving_pack = jnp.concatenate([leaving_state, leaving_factor[:, None, :]], axis=1)
    prefix = passed_along(leaving_pack, "group", 1)
    distance = 1
    while distance < group_count - 1:
        earlier = passed_along(prefix, "group", distance)
        prefix = jnp.concatenate(
            [
                prefix[:, ATTENTION_DEPTH:, :][:, :, :, None].squeeze(1) * earlier[:, :ATTENTION_DEPTH, :]
                + prefix[:, :ATTENTION_DEPTH, :],
                prefix[:, ATTENTION_DEPTH:, :] * earlier[:, ATTENTION_DEPTH:, :],
            ],
            axis=1,
        )
        distance *= 2
    incoming = prefix[:, :ATTENTION_DEPTH, :]
    block_out = block_out + jnp.einsum(
        "bhts,hsj->bhtj", carry_rows, incoming, precision=EXACT_ARITHMETIC
    )
    page_end = page_end + page_factor[:, :, :, None] * incoming[None]
    attended = block_out.transpose(0, 2, 1, 3).reshape(slot_rows, features_on_shard)
    normed = (group_norm(attended) * attender_scaling_coefs * gating).astype(jnp.bfloat16)
    head_count = lax.axis_size("head")
    mixer_partial = jnp.einsum(
        "rc,bfc->brf",
        normed,
        output_weight_t.reshape(head_count, -1, output_weight_t.shape[1]),
        preferred_element_type=jnp.float32,
    ).astype(jnp.bfloat16)
    mixer_owned = hier_reduce_scatter(mixer_partial, "head").astype(jnp.bfloat16)
    mixer_total = (
        hier_all_gather(mixer_owned, "head").transpose(1, 0, 2).reshape(slot_rows, full_width)
    ).astype(jnp.float32)
    residual = (embedded.astype(jnp.float32) + mixer_total).astype(jnp.bfloat16)
    last_residual = residual[slot_rows - 1 : slot_rows]
    arriving = passed_along(last_residual, "group", 1)
    channel_in = layer_norm(residual)
    channel_pages = channel_in.reshape(held, PAGE, full_width)
    edge_two = (
        jnp.concatenate([layer_norm(arriving), channel_pages[:-1, -1, :]], axis=0)
        * continues[:, None]
    )
    channel_prev = jnp.concatenate(
        [edge_two[:, None, :], channel_pages[:, :-1, :]], axis=1
    ).reshape(slot_rows, full_width)
    channel_delta = channel_prev - channel_in
    key_input = (channel_in + channel_delta * lag_blend_coefs[6]).astype(jnp.bfloat16)
    gate_input = (channel_in + channel_delta * lag_blend_coefs[7]).astype(jnp.bfloat16)
    gate_raw_two = jnp.dot(gate_input, projections[4], preferred_element_type=jnp.float32)
    key_raw = jnp.dot(key_input, key_weight, preferred_element_type=jnp.float32)
    squared = jnp.square(jax.nn.relu(key_raw)).astype(jnp.bfloat16)
    channel = hier_reduce_scatter(
        jnp.einsum(
            "rk,bfk->brf",
            squared,
            value_weight_t.reshape(head_count, -1, value_weight_t.shape[1]),
            preferred_element_type=jnp.float32,
        ).astype(jnp.bfloat16),
        "head",
    )
    gate_two = jax.nn.sigmoid(gate_raw_two)
    residual_local = lax.dynamic_slice_in_dim(
        residual, head_here * features_on_shard, features_on_shard, 1
    )
    hidden = (residual_local.astype(jnp.float32) + gate_two * channel).astype(jnp.bfloat16)
    state_held = page_end.reshape(held, attenders_on_shard, ATTENTION_DEPTH * ATTENTION_DEPTH)
    first_edge = lax.dynamic_slice_in_dim(
        current_pages[:, -1, :], head_here * features_on_shard, features_on_shard, 1
    )
    second_edge = lax.dynamic_slice_in_dim(
        channel_pages[:, -1, :], head_here * features_on_shard, features_on_shard, 1
    )
    edge_held = jnp.stack([first_edge, second_edge], axis=1)
    reach = 2
    shifts = range(-reach, reach + 1)

    def from_neighbours(value):
        return jnp.concatenate(
            [value if shift == 0 else passed_along(value, "group", -shift) for shift in shifts], axis=0
        )

    hidden_near = from_neighbours(hidden.reshape(held, PAGE, features_on_shard))
    state_near = from_neighbours(state_held)
    edge_near = from_neighbours(edge_held)
    slot_page = first_page + slot_number
    source_group = slot_page // held
    source_index = (source_group - group_here + reach) * held + slot_page - source_group * held
    source_index = jnp.clip(source_index, 0, (2 * reach + 1) * held - 1)
    hidden_out = jnp.take(hidden_near, source_index, axis=0)
    hidden_out = jnp.where(slot_live[:, None, None], hidden_out, jnp.zeros_like(hidden_out))
    hidden_out = hidden_out.reshape(SLOTS * PAGE, features_on_shard)
    state_out = jnp.take(state_near, source_index, axis=0)
    state_out = jnp.where(slot_live[:, None, None], state_out, jnp.zeros_like(state_out))
    edge_out = jnp.take(edge_near, source_index, axis=0)
    edge_out = jnp.where(slot_live[:, None, None], edge_out, jnp.zeros_like(edge_out))
    return (hidden_out, state_out, edge_out)


def solution(mesh):
    in_specs = (
        P(None, "head"),
        P(None, "group", "head"),
        P("group", "head"),
        P("head", "group"),
        P("head", "group"),
        P(),
        P(),
        P(),
        P(),
        P(None, "head"),
        P("head"),
        P("head"),
        P("head"),
        P(),
        P(),
        P(),
    )
    out_specs = (P("group", "head"), P("group", "head", None), P("group", None, "head"))
    return jax.shard_map(
        per_device, mesh=mesh, in_specs=in_specs, out_specs=out_specs, check_vma=False
    )
```

```python
import jax
import jax.numpy as jnp
from jax import lax
from jax.sharding import PartitionSpec as P

ATTENTION_DEPTH = 64
PAGE = 256
SLOTS = 4
BLOCK = 128


EXACT_ARITHMETIC = lax.Precision.HIGHEST
LAYER_EPS = 1e-05
GROUP_EPS = 0.00064


def passed_along(value, axis, steps):
    count = lax.axis_size(axis)
    initial, last = (max(0, -steps), min(count, count - steps))
    return lax.ppermute(value, axis, [(source, source + steps) for source in range(initial, last)])


def _swap(value, axis, flip):
    count = lax.axis_size(axis)
    return lax.ppermute(value, axis, [(s, s ^ flip) for s in range(count)])


def _ring(value, axis, step):
    count = lax.axis_size(axis)
    pairs = []
    for s in range(count):
        z = (s // 2) % 4
        target = s - z * 2 + ((z + step) % 4) * 2
        pairs.append((s, target))
    return lax.ppermute(value, axis, pairs)


def hier_reduce_scatter(partial, axis):
    h = lax.axis_index(axis)
    core = h % 2
    z = (h // 2) % 4
    yh = h // 8
    _, rows, width = partial.shape
    blocks = partial.reshape(2, 4, 2, rows, width)
    mine = jnp.take(blocks, core, axis=2)
    other = jnp.take(blocks, 1 - core, axis=2)
    acc = (mine.astype(jnp.float32) + _swap(other, axis, 1).astype(jnp.float32)).astype(jnp.bfloat16)
    total = jnp.take(acc, z, axis=1).astype(jnp.float32)
    for step in (1, 2, 3):
        send = jnp.take(acc, (z + step) % 4, axis=1)
        total = total + _ring(send, axis, step).astype(jnp.float32)
    total = total.astype(jnp.bfloat16)
    keep = jnp.take(total, yh, axis=0)
    give = jnp.take(total, 1 - yh, axis=0)
    return keep.astype(jnp.float32) + _swap(give, axis, 8).astype(jnp.float32)


def hier_all_gather(piece, axis):
    h = lax.axis_index(axis)
    core = h % 2
    z = (h // 2) % 4
    yh = h // 8
    got = _swap(piece, axis, 8)
    pair = jnp.take(jnp.stack([piece, got]), (jnp.arange(2) - yh) % 2, axis=0)
    ring_parts = [pair] + [_ring(pair, axis, -step % 4) for step in (1, 2, 3)]
    stacked = jnp.stack(ring_parts, 1)
    by_z = jnp.take(stacked, (jnp.arange(4) - z) % 4, axis=1)
    partner = _swap(by_z, axis, 1)
    both = jnp.take(jnp.stack([by_z, partner], 2), (jnp.arange(2) - core) % 2, axis=2)
    return both.reshape((16,) + piece.shape)


def layer_norm(value_rows):
    value_rows = value_rows.astype(jnp.float32)
    centered = value_rows - jnp.mean(value_rows, axis=-1, keepdims=True)
    return centered * lax.rsqrt(jnp.mean(centered * centered, axis=-1, keepdims=True) + LAYER_EPS)


def mixed_inputs(current, previous, lag_blend_coefs, blend_narrowing_map, blend_widening_maps):
    delta_rows = previous - current
    seeded = (current + delta_rows * lag_blend_coefs[0]).astype(jnp.bfloat16)
    low_rank = jnp.tanh(
        jnp.dot(seeded, blend_narrowing_map, preferred_element_type=jnp.float32)
    ).astype(jnp.bfloat16)
    rank_width = blend_widening_maps.shape[1]
    result_lines = []
    for number in range(5):
        column_part = low_rank[:, number * rank_width : (number + 1) * rank_width]
        offset = jnp.dot(
            column_part, blend_widening_maps[number], preferred_element_type=jnp.float32
        )
        result_lines.append(
            (current + delta_rows * (lag_blend_coefs[number + 1] + offset)).astype(jnp.bfloat16)
        )
    return result_lines


def log_decay(mixed_decay, fading_narrowing_map, fading_widening_map, initial_fading_power):
    hidden_low = jnp.tanh(
        jnp.dot(mixed_decay, fading_narrowing_map, preferred_element_type=jnp.float32)
    ).astype(jnp.bfloat16)
    return -jnp.exp(
        initial_fading_power
        + jnp.dot(hidden_low, fading_widening_map, preferred_element_type=jnp.float32)
    )


def group_norm(value_rows):
    shaped = value_rows.reshape(value_rows.shape[0], -1, ATTENTION_DEPTH)
    centered = shaped - jnp.mean(shaped, axis=-1, keepdims=True)
    normed = centered * lax.rsqrt(jnp.mean(centered * centered, axis=-1, keepdims=True) + GROUP_EPS)
    return normed.reshape(value_rows.shape)


def per_device(
    symbol_lookup_table,
    joined_linear_maps,
    feedforward_lookup_map,
    timeblend_result_map,
    feedforward_content_map,
    lag_blend_coefs,
    blend_narrowing_map,
    blend_widening_maps,
    fading_narrowing_map,
    fading_widening_map,
    initial_fading_power,
    present_symbol_extra,
    attender_scaling_coefs,
    active_cluster_sheets,
    sheets_for_inquiry,
    sheet_symbol_indices,
):
    group_count = lax.axis_size("group")
    group_here = lax.axis_index("group")
    head_here = lax.axis_index("head")
    features_on_shard = present_symbol_extra.shape[0]
    attenders_on_shard = features_on_shard // ATTENTION_DEPTH
    held = sheet_symbol_indices.shape[0] // group_count
    slot_rows = held * PAGE
    full_width = lag_blend_coefs.shape[1]
    group_number = jnp.arange(group_count, dtype=jnp.int32)
    pick_group = group_number == group_here
    live_count = jnp.sum(jnp.where(pick_group, active_cluster_sheets, 0))
    group_first = jnp.cumsum(active_cluster_sheets) - active_cluster_sheets
    first_page = jnp.sum(jnp.where(pick_group, group_first, 0))
    slot_number = jnp.arange(SLOTS, dtype=jnp.int32)
    slot_live = slot_number < live_count
    held_number = jnp.arange(held, dtype=jnp.int32)
    request_first = jnp.cumsum(sheets_for_inquiry) - sheets_for_inquiry
    page_here = group_here * held + held_number
    begins = jnp.any(page_here[:, None] == request_first[None, :], axis=1)
    continues = jnp.where(jnp.logical_not(begins), 1.0, 0.0).astype(jnp.float32)
    tokens_here = jnp.take(sheet_symbol_indices, page_here, axis=0)
    before_token = jnp.take(sheet_symbol_indices[:, -1], jnp.maximum(page_here - 1, 0))
    edge_pad = jnp.concatenate([before_token, jnp.zeros((8 - held,), before_token.dtype)])
    all_tokens = jnp.concatenate([tokens_here.reshape(-1), edge_pad])
    own_rows = jnp.take(symbol_lookup_table, all_tokens, axis=0)
    gathered_rows = lax.all_gather(own_rows, "head", axis=1, tiled=True)
    embedded = gathered_rows[:slot_rows]
    edge_rows = gathered_rows[slot_rows : slot_rows + held]
    map_count = joined_linear_maps.shape[0]
    first_pack = jnp.concatenate(
        [joined_linear_maps, timeblend_result_map.T[None]], axis=0
    ).astype(jnp.bfloat16)
    second_pack = jnp.stack(
        [feedforward_lookup_map, feedforward_content_map.T], axis=0
    ).astype(jnp.bfloat16)
    first_pack, _ = lax.optimization_barrier((first_pack, gathered_rows))
    first_full = lax.all_gather(first_pack, "group", axis=1, tiled=True)
    second_pack, _ = lax.optimization_barrier((second_pack, first_full))
    second_full = lax.all_gather(second_pack, "group", axis=1, tiled=True)
    projections = first_full[:map_count]
    output_weight_t = first_full[map_count]
    key_weight = second_full[0]
    value_weight_t = second_full[1]
    current = layer_norm(embedded)
    edge_first = layer_norm(edge_rows) * continues[:, None]
    current_pages = current.reshape(held, PAGE, full_width)
    previous = jnp.concatenate([edge_first[:, None, :], current_pages[:, :-1, :]], axis=1).reshape(
        slot_rows, full_width
    )
    mixed_decay, mixed_key, mixed_value, mixed_query, mixed_gate = mixed_inputs(
        current, previous, lag_blend_coefs, blend_narrowing_map, blend_widening_maps
    )
    fading_multipliers = log_decay(
        mixed_decay, fading_narrowing_map, fading_widening_map, initial_fading_power
    )
    acceptance_lines = jnp.dot(mixed_query, projections[0], preferred_element_type=jnp.float32)
    present_lookups = jnp.dot(mixed_key, projections[1], preferred_element_type=jnp.float32)
    present_contents = jnp.dot(mixed_value, projections[2], preferred_element_type=jnp.float32)
    gate_raw = jnp.dot(mixed_gate, projections[3], preferred_element_type=jnp.float32)
    gating = jax.nn.silu(gate_raw)
    blocks = slot_rows // BLOCK
    per_page = PAGE // BLOCK

    def to_blocks(value_rows):
        return value_rows.reshape(blocks, BLOCK, attenders_on_shard, ATTENTION_DEPTH).transpose(
            0, 2, 1, 3
        )

    block_index = jnp.arange(blocks, dtype=jnp.int32)
    block_start = block_index % per_page == 0
    block_slot = block_index // per_page
    slot_keep = continues * (held_number > 0)
    keep_state = jnp.where(block_start, jnp.take(slot_keep, block_slot), 1.0)
    keep_factor = jnp.where(block_start, jnp.take(continues, block_slot), 1.0)
    attender_extra = present_symbol_extra.reshape(attenders_on_shard, ATTENTION_DEPTH)
    strictly_lower = jnp.arange(BLOCK)[:, None] > jnp.arange(BLOCK)[None, :]

    askers_b = to_blocks(acceptance_lines)
    lookups_b = to_blocks(present_lookups)
    values_b = to_blocks(present_contents)
    decay_b = to_blocks(fading_multipliers)
    inclusive = jnp.cumsum(decay_b, axis=2)
    exclusive = inclusive - decay_b
    query_scaled = askers_b * jnp.exp(exclusive)
    key_scaled = lookups_b * jnp.exp(-inclusive)
    scores = jnp.einsum("bhts,bhus->bhtu", query_scaled, key_scaled, precision=EXACT_ARITHMETIC)
    scores = jnp.where(strictly_lower, scores, 0.0)
    selfpair_contribution = jnp.sum(askers_b * attender_extra[None, :, None, :] * lookups_b, axis=3)
    intra = (
        jnp.einsum("bhtu,bhuj->bhtj", scores, values_b, precision=EXACT_ARITHMETIC)
        + selfpair_contribution[..., None] * values_b
    )
    block_total = inclusive[:, :, -1, :]
    block_decay = jnp.exp(block_total)
    key_end = lookups_b * jnp.exp(block_total[:, :, None, :] - inclusive)
    block_kv = jnp.einsum("bhts,bhtj->bhsj", key_end, values_b, precision=EXACT_ARITHMETIC)
    sweep = jnp.zeros((attenders_on_shard, ATTENTION_DEPTH, ATTENTION_DEPTH), jnp.float32)
    factor = jnp.ones((attenders_on_shard, ATTENTION_DEPTH), jnp.float32)
    starts, factors_before, ends, factors_after = [], [], [], []
    for number in range(blocks):
        sweep = sweep * keep_state[number]
        factor = factor * keep_factor[number]
        starts.append(sweep)
        factors_before.append(factor)
        sweep = block_decay[number][:, :, None] * sweep + block_kv[number]
        factor = factor * block_decay[number]
        ends.append(sweep)
        factors_after.append(factor)
    block_out = intra + jnp.einsum(
        "bhts,bhsj->bhtj", query_scaled, jnp.stack(starts), precision=EXACT_ARITHMETIC
    )
    carry_rows = query_scaled * jnp.stack(factors_before)[:, :, None, :]
    block_states = jnp.stack(ends)
    block_factors = jnp.stack(factors_after)
    page_end = block_states[per_page - 1 :: per_page]
    page_factor = block_factors[per_page - 1 :: per_page]
    leaving_state = page_end[-1]
    leaving_factor = page_factor[-1]

    leaving_pack = jnp.concatenate([leaving_state, leaving_factor[:, None, :]], axis=1)
    arrivals = [passed_along(leaving_pack, "group", distance) for distance in range(1, group_count)]
    incoming = jnp.zeros_like(leaving_state)
    for arrival in reversed(arrivals):
        incoming = arrival[:, ATTENTION_DEPTH, :][:, :, None] * incoming + arrival[:, :ATTENTION_DEPTH, :]
    block_out = block_out + jnp.einsum(
        "bhts,hsj->bhtj", carry_rows, incoming, precision=EXACT_ARITHMETIC
    )
    page_end = page_end + page_factor[:, :, :, None] * incoming[None]
    attended = block_out.transpose(0, 2, 1, 3).reshape(slot_rows, features_on_shard)
    normed = (group_norm(attended) * attender_scaling_coefs * gating).astype(jnp.bfloat16)
    head_count = lax.axis_size("head")
    mixer_partial = jnp.einsum(
        "rc,bfc->brf",
        normed,
        output_weight_t.reshape(head_count, -1, output_weight_t.shape[1]),
        preferred_element_type=jnp.float32,
    ).astype(jnp.bfloat16)
    mixer_owned = hier_reduce_scatter(mixer_partial, "head").astype(jnp.bfloat16)
    mixer_total = (
        hier_all_gather(mixer_owned, "head").transpose(1, 0, 2).reshape(slot_rows, full_width)
    ).astype(jnp.float32)
    residual = (embedded.astype(jnp.float32) + mixer_total).astype(jnp.bfloat16)
    last_residual = residual[slot_rows - 1 : slot_rows]
    arriving = passed_along(last_residual, "group", 1)
    channel_in = layer_norm(residual)
    channel_pages = channel_in.reshape(held, PAGE, full_width)
    edge_two = (
        jnp.concatenate([layer_norm(arriving), channel_pages[:-1, -1, :]], axis=0)
        * continues[:, None]
    )
    channel_prev = jnp.concatenate(
        [edge_two[:, None, :], channel_pages[:, :-1, :]], axis=1
    ).reshape(slot_rows, full_width)
    channel_delta = channel_prev - channel_in
    key_input = (channel_in + channel_delta * lag_blend_coefs[6]).astype(jnp.bfloat16)
    gate_input = (channel_in + channel_delta * lag_blend_coefs[7]).astype(jnp.bfloat16)
    gate_raw_two = jnp.dot(gate_input, projections[4], preferred_element_type=jnp.float32)
    key_raw = jnp.dot(key_input, key_weight, preferred_element_type=jnp.float32)
    squared = jnp.square(jax.nn.relu(key_raw)).astype(jnp.bfloat16)
    channel = hier_reduce_scatter(
        jnp.einsum(
            "rk,bfk->brf",
            squared,
            value_weight_t.reshape(head_count, -1, value_weight_t.shape[1]),
            preferred_element_type=jnp.float32,
        ).astype(jnp.bfloat16),
        "head",
    )
    gate_two = jax.nn.sigmoid(gate_raw_two)
    residual_local = lax.dynamic_slice_in_dim(
        residual, head_here * features_on_shard, features_on_shard, 1
    )
    hidden = (residual_local.astype(jnp.float32) + gate_two * channel).astype(jnp.bfloat16)
    state_held = page_end.reshape(held, attenders_on_shard, ATTENTION_DEPTH * ATTENTION_DEPTH)
    first_edge = lax.dynamic_slice_in_dim(
        current_pages[:, -1, :], head_here * features_on_shard, features_on_shard, 1
    )
    second_edge = lax.dynamic_slice_in_dim(
        channel_pages[:, -1, :], head_here * features_on_shard, features_on_shard, 1
    )
    edge_held = jnp.stack([first_edge, second_edge], axis=1)
    reach = 2
    shifts = range(-reach, reach + 1)

    def from_neighbours(value):
        return jnp.concatenate(
            [value if shift == 0 else passed_along(value, "group", -shift) for shift in shifts], axis=0
        )

    hidden_near = from_neighbours(hidden.reshape(held, PAGE, features_on_shard))
    state_near = from_neighbours(state_held)
    edge_near = from_neighbours(edge_held)
    slot_page = first_page + slot_number
    source_group = slot_page // held
    source_index = (source_group - group_here + reach) * held + slot_page - source_group * held
    source_index = jnp.clip(source_index, 0, (2 * reach + 1) * held - 1)
    hidden_out = jnp.take(hidden_near, source_index, axis=0)
    hidden_out = jnp.where(slot_live[:, None, None], hidden_out, jnp.zeros_like(hidden_out))
    hidden_out = hidden_out.reshape(SLOTS * PAGE, features_on_shard)
    state_out = jnp.take(state_near, source_index, axis=0)
    state_out = jnp.where(slot_live[:, None, None], state_out, jnp.zeros_like(state_out))
    edge_out = jnp.take(edge_near, source_index, axis=0)
    edge_out = jnp.where(slot_live[:, None, None], edge_out, jnp.zeros_like(edge_out))
    return (hidden_out, state_out, edge_out)


def solution(mesh):
    in_specs = (
        P(None, "head"),
        P(None, "group", "head"),
        P("group", "head"),
        P("head", "group"),
        P("head", "group"),
        P(),
        P(),
        P(),
        P(),
        P(None, "head"),
        P("head"),
        P("head"),
        P("head"),
        P(),
        P(),
        P(),
    )
    out_specs = (P("group", "head"), P("group", "head", None), P("group", None, "head"))
    return jax.shard_map(
        per_device, mesh=mesh, in_specs=in_specs, out_specs=out_specs, check_vma=False
    )
```
